128 devices in a mesh: dev: 128 (over z, x, y, core).
Axes of the slice: x: 4, y: 4, z: 4, core: 2. Of those that a mesh axis runs over, the one named last changes fastest.
Arguments:
- cotangent: float32 [8192, 3, 576], P('dev'), may hold values from -6 to 6
- surface: float32 [8192, 3, 576], P('dev'), may hold values from -0.9 to 0.9
- region_id: int32 [8192], P('dev'), may hold values from 0 to 63
- local_target: int32 [8192], P('dev'), may hold values from 0 to 63
- local_shift: int32 [8192], P('dev'), may hold values from 1 to 63
- near_target: int32 [128, 128, 2], P('dev'), may hold values from 0 to 63
- near_source: int32 [128, 128, 2], P('dev'), may hold values from 0 to 63
- near_count: int32 [128, 128], P('dev'), may hold values from 0 to 2
Outputs:
- grad_density: float32 [8192, 3, 576], P('dev')
The draws below stay inside these ranges and needn't reach their ends.
Inputs may be any that keep to these rules, and one draw needn't show every extreme that they name: Only slots c < near_count[d, p] are pairs; the others of near_target and near_source are not.
All inputs are finite; a program needn't handle non-finite values.
Results may differ from the reference program's by a relative error of at most 0.0003.
Values sent between devices are 32-bit elements; how exact they have to be, the bound alone decides.
No kernel may reach another device: no remote copies, remote signals or barrier semaphores. Data moves between devices by JAX's collectives and lax.ppermute only.
A program may use at most 64 MiB of HBM per device.

```python
import math
import jax
import jax.numpy as jnp
from jax import lax

NLAT = 24
COEF = 576
NEAR_LAT = 8
NEAR_POINTS = 128
VES_DEV = 64
CAP = 2
REGIONS = 64
FAR = 8
NVES = 8192
N_DEV = 128


def plant(result, stream_key, least, top_value):
    longest = result.shape.index(max(result.shape))
    spots = []
    for shift in (0, 1):
        where = [jax.random.randint(jax.random.fold_in(stream_key, axis), (), 0, length) for axis, length in enumerate(result.shape)]
        where[longest] = (where[longest] + shift) % result.shape[longest]
        spots.append(tuple(where))
    return result.at[spots[0]].set(least).at[spots[1]].set(top_value)


def levels(own_key, dims, pieces, least, largest):
    level = 1.0
    for dim, blocks in pieces:
        draws = jax.random.uniform(jax.random.fold_in(jax.random.fold_in(own_key, 6), dim), (blocks,), jnp.float32, least / len(pieces), largest / len(pieces))
        level = level * jnp.repeat(jnp.exp(draws), dims[dim] // blocks).reshape((-1,) + (1,) * (len(dims) - 1 - dim))
    return level


def bell_draw(stream_key, shape, scale, reach, shards=(), held_as=jnp.bfloat16):
    values = scale * jax.random.normal(stream_key, shape, jnp.float32)
    if shards:
        values = values * levels(stream_key, shape, shards, -0.22, 0.18)
    return jnp.clip(values, -reach, reach).astype(held_as)


def setup_inputs(seed: int = 0) -> dict:
    keys = jax.random.split(jax.random.key(seed), 9)
    return {
        "cotangent": bell_draw(keys[0], (NVES, 3, COEF), 1.0, 6.0, ((0, 128),), jnp.float32),
        "surface": bell_draw(keys[1], (NVES, 3, COEF), 0.15, 0.9, ((0, 128),), jnp.float32),
        "region_id": plant(jax.random.randint(keys[2], (NVES,), 0, REGIONS), jax.random.fold_in(keys[2], 1), 0, REGIONS - 1).astype(jnp.int32),
        "local_target": plant(jax.random.randint(keys[3], (NVES,), 0, VES_DEV), jax.random.fold_in(keys[3], 1), 0, VES_DEV - 1).astype(jnp.int32),
        "local_shift": plant(jax.random.randint(keys[4], (NVES,), 1, VES_DEV), jax.random.fold_in(keys[4], 1), 1, VES_DEV - 1).astype(jnp.int32),
        "near_target": plant(jax.random.randint(keys[5], (N_DEV, N_DEV, CAP), 0, VES_DEV), jax.random.fold_in(keys[5], 1), 0, VES_DEV - 1).astype(jnp.int32),
        "near_source": plant(jax.random.randint(keys[6], (N_DEV, N_DEV, CAP), 0, VES_DEV), jax.random.fold_in(keys[6], 1), 0, VES_DEV - 1).astype(jnp.int32),
        "near_count": plant(jax.random.randint(keys[7], (N_DEV, N_DEV), 0, CAP + 1), jax.random.fold_in(keys[7], 1), 0, CAP).astype(jnp.int32),
    }


HIGHEST = lax.Precision.HIGHEST

def harmonic_tables(grid_lat, degree_count):
    longitudes = 2 * grid_lat
    full_longitudes = 2 * degree_count
    colatitude = (jnp.arange(grid_lat, dtype=jnp.float32) + 0.5) * (math.pi / grid_lat)
    cosine = jnp.cos(colatitude)
    values = [jnp.ones_like(cosine), cosine]
    for degree in range(2, degree_count):
        values.append(((2 * degree - 1) * cosine * values[-1] - (degree - 1) * values[-2]) / degree)
    degrees = jnp.arange(degree_count, dtype=jnp.float32)
    legendre = jnp.stack(values[:degree_count], axis=1) * jnp.sqrt((2.0 * degrees + 1.0) / 2.0)
    azimuth = jnp.arange(longitudes, dtype=jnp.float32) * (2.0 * math.pi / longitudes)
    halfway = degree_count // 2
    mode_index = jnp.arange(degree_count, dtype=jnp.float32)
    frequency = jnp.where(mode_index < halfway, mode_index, mode_index - halfway + 1.0)
    phases = azimuth[:, None] * frequency[None, :]
    fourier = jnp.where(mode_index[None, :] < halfway, jnp.cos(phases), jnp.sin(phases))
    fourier = fourier * jnp.where(mode_index[None, :] == 0, math.sqrt(1.0 / full_longitudes), math.sqrt(2.0 / full_longitudes))
    synthesis = jnp.einsum('jl,km->lmjk', legendre, fourier).reshape(degree_count * degree_count, grid_lat * longitudes)
    quadrature = jnp.repeat(jnp.sin(colatitude) * (math.pi / grid_lat), longitudes)
    analysis = (synthesis * quadrature[None, :]).T
    degree_scale = jnp.repeat(1.0 / (2.0 * degrees + 1.0), degree_count)
    return (synthesis, analysis, degree_scale)

def far_coupling(regions, vesicle_total):
    position = jnp.arange(regions, dtype=jnp.float32)
    return 1.0 / ((1.0 + jnp.abs(position[:, None] - position[None, :])) * math.sqrt(vesicle_total))

def to_points(coefs, synthesis):
    count_rows = coefs.shape[0]
    flattened = coefs.reshape(count_rows * coefs.shape[1], coefs.shape[2])
    return jnp.dot(flattened, synthesis, precision=HIGHEST).reshape(count_rows, coefs.shape[1], synthesis.shape[1])

def to_coefs(points, analysis):
    count_rows = points.shape[0]
    flattened = points.reshape(count_rows * points.shape[1], points.shape[2])
    return jnp.dot(flattened, analysis, precision=HIGHEST).reshape(count_rows, points.shape[1], analysis.shape[1])

def pair_terms(target_shapes, source_shapes, target_cots):
    distance = jnp.zeros((target_shapes.shape[0], target_shapes.shape[2], source_shapes.shape[2]), jnp.float32)
    for component in range(3):
        apart = target_shapes[:, component, :, None] - source_shapes[:, component, None, :]
        distance = distance + apart * apart
    kernel_block = 1.0 / (1.0 + distance)
    scale = 1.0 / math.sqrt(target_shapes.shape[2])
    return jnp.einsum('pca,pab->pcb', target_cots, kernel_block, precision=HIGHEST) * scale

def reference(cotangent, surface, region_id, local_target, local_shift, near_target, near_source, near_count):
    synthesis, analysis, degree_scale = harmonic_tables(NLAT, NLAT)
    near_synthesis, near_analysis, unused_scale = harmonic_tables(NEAR_LAT, NLAT)
    cot_points = to_points(cotangent, synthesis)
    shape_points = to_points(surface, synthesis)
    near_cot = to_points(cotangent, near_synthesis)
    near_shape = to_points(surface, near_synthesis)
    stretch = 1.0 / (1.0 + lax.optimization_barrier(jnp.sum(shape_points * shape_points, axis=1)))
    point_total = stretch[:, None, :] * cot_points
    slot_index = jnp.arange(CAP, dtype=jnp.int32)
    peer_offset = jnp.arange(N_DEV, dtype=jnp.int32)[:, None] * VES_DEV

    def one_device(accumulated, device):
        offset = device * VES_DEV
        here_target = lax.dynamic_slice_in_dim(local_target, offset, VES_DEV)
        here_shift = lax.dynamic_slice_in_dim(local_shift, offset, VES_DEV)
        target_all = jnp.concatenate([offset + here_target, (offset + near_target[device]).reshape(-1)])
        source_all = jnp.concatenate([offset + (here_target + here_shift) % VES_DEV, (peer_offset + near_source[:, device, :]).reshape(-1)])
        alive_mask = jnp.concatenate([jnp.ones((VES_DEV,), jnp.float32), (slot_index[None, :] < near_count[device][:, None]).astype(jnp.float32).reshape(-1)])
        terms = pair_terms(near_shape[target_all], near_shape[source_all], near_cot[target_all])
        return (accumulated.at[source_all].add(alive_mask[:, None, None] * terms), None)
    near_start = jnp.zeros((NVES, 3, NEAR_POINTS), jnp.float32)
    near_total, unused = lax.scan(one_device, near_start, jnp.arange(N_DEV, dtype=jnp.int32))
    gradient = degree_scale * cotangent + to_coefs(point_total, analysis) + to_coefs(near_total, near_analysis)
    member = (region_id[:, None] == jnp.arange(REGIONS, dtype=jnp.int32)[None, :]).astype(jnp.float32)
    far_total = jnp.dot(member.T, cotangent[:, :, :FAR].reshape(NVES, 3 * FAR), precision=HIGHEST)
    far_field = jnp.dot(far_coupling(REGIONS, NVES).T, far_total, precision=HIGHEST)
    far_terms = jnp.dot(member, far_field, precision=HIGHEST).reshape(NVES, 3, FAR)
    return gradient + jnp.pad(far_terms, ((0, 0), (0, 0), (0, COEF - FAR)))
```

```python
import math

import jax
import jax.numpy as jnp
import numpy as np
from jax import lax
from jax.sharding import PartitionSpec as P

NLAT = 24
NEAR_LAT = 8
REGIONS = 64
FAR = 8


HIGHEST = lax.Precision.HIGHEST


def harmonic_tables(grid_lat, degree_count):
    longitudes = 2 * grid_lat
    full_longitudes = 2 * degree_count
    colatitude = (np.arange(grid_lat, dtype=np.float64) + 0.5) * (math.pi / grid_lat)
    cosine = np.cos(colatitude)
    values = [np.ones_like(cosine), cosine]
    for degree in range(2, degree_count):
        values.append(((2 * degree - 1) * cosine * values[-1] - (degree - 1) * values[-2]) / degree)
    degrees = np.arange(degree_count, dtype=np.float64)
    legendre = np.stack(values[:degree_count], axis=1) * np.sqrt((2.0 * degrees + 1.0) / 2.0)
    azimuth = np.arange(longitudes, dtype=np.float64) * (2.0 * math.pi / longitudes)
    halfway = degree_count // 2
    mode_index = np.arange(degree_count, dtype=np.float64)
    frequency = np.where(mode_index < halfway, mode_index, mode_index - halfway + 1.0)
    phases = azimuth[:, None] * frequency[None, :]
    fourier = np.where(mode_index[None, :] < halfway, np.cos(phases), np.sin(phases))
    fourier = fourier * np.where(
        mode_index[None, :] == 0, math.sqrt(1.0 / full_longitudes), math.sqrt(2.0 / full_longitudes)
    )
    synthesis = np.einsum("jl,km->lmjk", legendre, fourier).reshape(
        degree_count * degree_count, grid_lat * longitudes
    )
    quadrature = np.repeat(np.sin(colatitude) * (math.pi / grid_lat), longitudes)
    degree_scale = np.repeat(1.0 / (2.0 * degrees + 1.0), degree_count)
    return (synthesis, quadrature, degree_scale)


def far_coupling(regions, vesicle_total):
    position = np.arange(regions, dtype=np.float64)
    return 1.0 / ((1.0 + np.abs(position[:, None] - position[None, :])) * math.sqrt(vesicle_total))


def pair_terms(target_shapes, source_shapes, target_cots):
    distance = jnp.zeros(
        (target_shapes.shape[0], target_shapes.shape[2], source_shapes.shape[2]), jnp.float32
    )
    for component in range(3):
        apart = target_shapes[:, component, :, None] - source_shapes[:, component, None, :]
        distance = distance + apart * apart
    kernel_block = 1.0 / (1.0 + distance)
    scale = 1.0 / math.sqrt(target_shapes.shape[2])
    return jnp.einsum("pca,pab->pcb", target_cots, kernel_block, precision=HIGHEST) * scale


def onehot(index, count):
    return (index[:, None] == jnp.arange(count, dtype=jnp.int32)[None, :]).astype(jnp.float32)


def on_device(
    cotangent, surface, region_id, local_target, local_shift, near_target, near_source, near_count
):
    vesicles = cotangent.shape[0]
    coef_count = cotangent.shape[2]
    devices = lax.axis_size("dev")
    slot_count = near_target.shape[2]
    pair_slots = devices * slot_count

    synthesis, quadrature, degree_scale = harmonic_tables(NLAT, NLAT)
    near_synthesis, near_quadrature, unused_scale = harmonic_tables(NEAR_LAT, NLAT)
    points = synthesis.shape[1]
    near_points = near_synthesis.shape[1]
    both = jnp.asarray(np.concatenate([synthesis, near_synthesis], axis=1).astype(np.float32))
    weights = jnp.asarray(np.concatenate([quadrature, near_quadrature]).astype(np.float32))

    cot_all = jnp.dot(
        cotangent.reshape(vesicles * 3, coef_count), both, precision=HIGHEST
    ).reshape(vesicles, 3, points + near_points)
    shape_all = jnp.dot(
        surface.reshape(vesicles * 3, coef_count), both, precision=HIGHEST
    ).reshape(vesicles, 3, points + near_points)
    cot_points = cot_all[:, :, :points]
    near_cot = cot_all[:, :, points:]
    shape_points = shape_all[:, :, :points]
    near_shape = shape_all[:, :, points:]
    stretch = 1.0 / (1.0 + jnp.sum(shape_points * shape_points, axis=1))
    point_total = stretch[:, None, :] * cot_points

    near_width = 3 * near_points
    shape_rows = near_shape.reshape(vesicles, near_width)
    cot_rows = near_cot.reshape(vesicles, near_width)
    target_rows = jnp.concatenate([shape_rows, cot_rows], axis=1)

    targets = near_target[0].reshape(pair_slots)
    alive = (
        jnp.arange(slot_count, dtype=jnp.int32)[None, :] < near_count[0][:, None]
    ).reshape(pair_slots)
    picked = jnp.dot(onehot(targets, vesicles), target_rows, precision=HIGHEST)
    outgoing = jnp.concatenate(
        [picked[:, :near_width], jnp.where(alive[:, None], picked[:, near_width:], 0.0)], axis=1
    ).reshape(devices, slot_count, 2 * near_width)
    incoming = lax.all_to_all(outgoing, "dev", split_axis=0, concat_axis=0, tiled=True).reshape(
        pair_slots, 2 * near_width
    )
    sources = near_source[0].reshape(pair_slots)
    source_onehot = onehot(sources, vesicles)

    local_source = (local_target + local_shift) % vesicles
    local_onehot = onehot(local_source, vesicles)
    local_picked = jnp.dot(onehot(local_target, vesicles), target_rows, precision=HIGHEST)
    local_terms = pair_terms(
        local_picked[:, :near_width].reshape(vesicles, 3, near_points),
        jnp.dot(local_onehot, shape_rows, precision=HIGHEST).reshape(vesicles, 3, near_points),
        local_picked[:, near_width:].reshape(vesicles, 3, near_points),
    )
    remote_terms = pair_terms(
        incoming[:, :near_width].reshape(pair_slots, 3, near_points),
        jnp.dot(source_onehot, shape_rows, precision=HIGHEST).reshape(pair_slots, 3, near_points),
        incoming[:, near_width:].reshape(pair_slots, 3, near_points),
    )
    contract_rows = (((0,), (0,)), ((), ()))
    near_total = lax.dot_general(
        local_onehot, local_terms.reshape(vesicles, near_width), contract_rows, precision=HIGHEST
    ) + lax.dot_general(
        source_onehot, remote_terms.reshape(pair_slots, near_width), contract_rows, precision=HIGHEST
    )

    weighted = jnp.concatenate(
        [point_total, near_total.reshape(vesicles, 3, near_points)], axis=2
    ) * weights
    analysed = lax.dot_general(
        weighted.reshape(vesicles * 3, points + near_points),
        both,
        (((1,), (1,)), ((), ())),
        precision=HIGHEST,
    ).reshape(cotangent.shape)
    gradient = jnp.asarray(degree_scale.astype(np.float32)) * cotangent + analysed

    member = onehot(region_id, REGIONS)
    moments = cotangent[:, :, :FAR].reshape(vesicles, 3 * FAR)
    partial_far = lax.dot_general(member, moments, contract_rows, precision=HIGHEST)
    far_total = jnp.sum(lax.all_gather(partial_far, "dev"), axis=0)
    coupling = jnp.asarray(far_coupling(REGIONS, vesicles * devices).astype(np.float32))
    far_field = lax.dot_general(coupling, far_total, contract_rows, precision=HIGHEST)
    far_terms = jnp.dot(member, far_field, precision=HIGHEST).reshape(vesicles, 3, FAR)
    return gradient + jnp.pad(far_terms, ((0, 0), (0, 0), (0, coef_count - FAR)))


def solution(mesh):
    in_specs = (
        P("dev", None, None),
        P("dev", None, None),
        P("dev"),
        P("dev"),
        P("dev"),
        P("dev", None, None),
        P("dev", None, None),
        P("dev", None),
    )
    out_specs = P("dev", None, None)
    return jax.shard_map(
        on_device, mesh=mesh, in_specs=in_specs, out_specs=out_specs, check_vma=False
    )
```

```python
import math

import jax
import jax.numpy as jnp
import numpy as np
from jax import lax
from jax.sharding import PartitionSpec as P

NLAT = 24
NEAR_LAT = 8
REGIONS = 64
FAR = 8


HIGHEST = lax.Precision.HIGHEST


def harmonic_tables(grid_lat, degree_count):
    longitudes = 2 * grid_lat
    full_longitudes = 2 * degree_count
    colatitude = (np.arange(grid_lat, dtype=np.float64) + 0.5) * (math.pi / grid_lat)
    cosine = np.cos(colatitude)
    values = [np.ones_like(cosine), cosine]
    for degree in range(2, degree_count):
        values.append(((2 * degree - 1) * cosine * values[-1] - (degree - 1) * values[-2]) / degree)
    degrees = np.arange(degree_count, dtype=np.float64)
    legendre = np.stack(values[:degree_count], axis=1) * np.sqrt((2.0 * degrees + 1.0) / 2.0)
    azimuth = np.arange(longitudes, dtype=np.float64) * (2.0 * math.pi / longitudes)
    halfway = degree_count // 2
    mode_index = np.arange(degree_count, dtype=np.float64)
    frequency = np.where(mode_index < halfway, mode_index, mode_index - halfway + 1.0)
    phases = azimuth[:, None] * frequency[None, :]
    fourier = np.where(mode_index[None, :] < halfway, np.cos(phases), np.sin(phases))
    fourier = fourier * np.where(
        mode_index[None, :] == 0, math.sqrt(1.0 / full_longitudes), math.sqrt(2.0 / full_longitudes)
    )
    synthesis = np.einsum("jl,km->lmjk", legendre, fourier).reshape(
        degree_count * degree_count, grid_lat * longitudes
    )
    quadrature = np.repeat(np.sin(colatitude) * (math.pi / grid_lat), longitudes)
    degree_scale = np.repeat(1.0 / (2.0 * degrees + 1.0), degree_count)
    return (synthesis, quadrature, degree_scale)


def far_coupling(regions, vesicle_total):
    position = np.arange(regions, dtype=np.float64)
    return 1.0 / ((1.0 + np.abs(position[:, None] - position[None, :])) * math.sqrt(vesicle_total))


def pair_terms(target_shapes, source_shapes, target_cots):
    distance = jnp.zeros(
        (target_shapes.shape[1], target_shapes.shape[2], source_shapes.shape[2]), jnp.float32
    )
    for component in range(3):
        apart = target_shapes[component, :, :, None] - source_shapes[component, :, None, :]
        distance = distance + apart * apart
    kernel_block = 1.0 / (1.0 + distance)
    scale = 1.0 / math.sqrt(target_shapes.shape[2])
    return jnp.einsum("cpa,pab->cpb", target_cots, kernel_block, precision=HIGHEST) * scale


def onehot(index, count):
    return (index[:, None] == jnp.arange(count, dtype=jnp.int32)[None, :]).astype(jnp.float32)


def on_device(
    cotangent, surface, region_id, local_target, local_shift, near_target, near_source, near_count
):
    vesicles = cotangent.shape[0]
    coef_count = cotangent.shape[2]
    devices = lax.axis_size("dev")
    slot_count = near_target.shape[2]
    pair_slots = devices * slot_count

    synthesis, quadrature, degree_scale = harmonic_tables(NLAT, NLAT)
    near_synthesis, near_quadrature, unused_scale = harmonic_tables(NEAR_LAT, NLAT)
    points = synthesis.shape[1]
    near_points = near_synthesis.shape[1]
    both = jnp.asarray(np.concatenate([synthesis, near_synthesis], axis=1).astype(np.float32))
    weights = jnp.asarray(np.concatenate([quadrature, near_quadrature]).astype(np.float32))
    contract_rows = (((0,), (0,)), ((), ()))

    cot_all = jnp.dot(
        cotangent.reshape(vesicles * 3, coef_count), both, precision=HIGHEST
    ).reshape(vesicles, 3, points + near_points)
    shape_all = jnp.dot(
        surface.reshape(vesicles * 3, coef_count), both, precision=HIGHEST
    ).reshape(vesicles, 3, points + near_points)
    cot_points = cot_all[:, :, :points]
    near_cot = cot_all[:, :, points:]
    shape_points = shape_all[:, :, :points]
    near_shape = shape_all[:, :, points:]
    stretch = 1.0 / (1.0 + jnp.sum(shape_points * shape_points, axis=1))
    point_total = stretch[:, None, :] * cot_points

    near_width = 3 * near_points
    near_rows = jnp.concatenate([near_shape, near_cot], axis=1).transpose(1, 0, 2)
    shape_rows = near_rows[:3]

    def pick(index, rows):
        return jnp.einsum("pv,kvx->kpx", onehot(index, vesicles), rows, precision=HIGHEST)

    targets = near_target[0].reshape(pair_slots)
    alive = (
        jnp.arange(slot_count, dtype=jnp.int32)[None, :] < near_count[0][:, None]
    ).reshape(pair_slots)
    picked = pick(targets, near_rows)
    kind = jnp.arange(6, dtype=jnp.int32)[:, None, None]
    picked = jnp.where((kind < 3) | alive[None, :, None], picked, 0.0)
    member = onehot(region_id, REGIONS)
    moments = cotangent[:, :, :FAR].reshape(vesicles, 3 * FAR)
    partial_far = lax.dot_general(member, moments, contract_rows, precision=HIGHEST)
    far_rows = partial_far.reshape(6, 1, slot_count, near_points)
    far_rows = jnp.broadcast_to(far_rows, (6, devices, slot_count, near_points)).reshape(
        6, pair_slots, near_points
    )
    outgoing = jnp.concatenate([picked, far_rows], axis=0)
    incoming = lax.all_to_all(outgoing, "dev", split_axis=1, concat_axis=1, tiled=True)
    far_total = jnp.sum(
        incoming[6:].reshape(6, devices, slot_count, near_points), axis=1
    ).reshape(REGIONS, 3 * FAR)
    sources = near_source[0].reshape(pair_slots)
    source_onehot = onehot(sources, vesicles)

    local_source = (local_target + local_shift) % vesicles
    local_onehot = onehot(local_source, vesicles)
    local_picked = pick(local_target, near_rows)
    local_terms = pair_terms(local_picked[:3], pick(local_source, shape_rows), local_picked[3:])
    remote_terms = pair_terms(incoming[:3], pick(sources, shape_rows), incoming[3:6])
    near_total = jnp.einsum(
        "pv,kpx->vkx", local_onehot, local_terms, precision=HIGHEST
    ) + jnp.einsum("pv,kpx->vkx", source_onehot, remote_terms, precision=HIGHEST)

    weighted = jnp.concatenate(
        [point_total, near_total.reshape(vesicles, 3, near_points)], axis=2
    ) * weights
    analysed = lax.dot_general(
        weighted.reshape(vesicles * 3, points + near_points),
        both,
        (((1,), (1,)), ((), ())),
        precision=HIGHEST,
    ).reshape(cotangent.shape)
    gradient = jnp.asarray(degree_scale.astype(np.float32)) * cotangent + analysed

    coupling = jnp.asarray(far_coupling(REGIONS, vesicles * devices).astype(np.float32))
    far_field = lax.dot_general(coupling, far_total, contract_rows, precision=HIGHEST)
    far_terms = jnp.dot(member, far_field, precision=HIGHEST).reshape(vesicles, 3, FAR)
    return gradient + jnp.pad(far_terms, ((0, 0), (0, 0), (0, coef_count - FAR)))


def solution(mesh):
    in_specs = (
        P("dev", None, None),
        P("dev", None, None),
        P("dev"),
        P("dev"),
        P("dev"),
        P("dev", None, None),
        P("dev", None, None),
        P("dev", None),
    )
    out_specs = P("dev", None, None)
    return jax.shard_map(
        on_device, mesh=mesh, in_specs=in_specs, out_specs=out_specs, check_vma=False
    )
```

```python
import math

import jax
import jax.numpy as jnp
import numpy as np
from jax import lax
from jax.experimental import pallas as pl
from jax.sharding import PartitionSpec as P

NLAT = 24
NEAR_LAT = 8
REGIONS = 64
FAR = 8


HIGHEST = lax.Precision.HIGHEST


def harmonic_tables(grid_lat, degree_count):
    longitudes = 2 * grid_lat
    full_longitudes = 2 * degree_count
    colatitude = (np.arange(grid_lat, dtype=np.float64) + 0.5) * (math.pi / grid_lat)
    cosine = np.cos(colatitude)
    values = [np.ones_like(cosine), cosine]
    for degree in range(2, degree_count):
        values.append(((2 * degree - 1) * cosine * values[-1] - (degree - 1) * values[-2]) / degree)
    degrees = np.arange(degree_count, dtype=np.float64)
    legendre = np.stack(values[:degree_count], axis=1) * np.sqrt((2.0 * degrees + 1.0) / 2.0)
    azimuth = np.arange(longitudes, dtype=np.float64) * (2.0 * math.pi / longitudes)
    halfway = degree_count // 2
    mode_index = np.arange(degree_count, dtype=np.float64)
    frequency = np.where(mode_index < halfway, mode_index, mode_index - halfway + 1.0)
    phases = azimuth[:, None] * frequency[None, :]
    fourier = np.where(mode_index[None, :] < halfway, np.cos(phases), np.sin(phases))
    fourier = fourier * np.where(
        mode_index[None, :] == 0, math.sqrt(1.0 / full_longitudes), math.sqrt(2.0 / full_longitudes)
    )
    synthesis = np.einsum("jl,km->lmjk", legendre, fourier).reshape(
        degree_count * degree_count, grid_lat * longitudes
    )
    quadrature = np.repeat(np.sin(colatitude) * (math.pi / grid_lat), longitudes)
    degree_scale = np.repeat(1.0 / (2.0 * degrees + 1.0), degree_count)
    return (synthesis, quadrature, degree_scale)


def far_coupling(regions, vesicle_total):
    position = np.arange(regions, dtype=np.float64)
    return 1.0 / ((1.0 + np.abs(position[:, None] - position[None, :])) * math.sqrt(vesicle_total))


GROUP = 8


def pair_kernel(t_ref, s_ref, c_ref, o_ref):
    block = t_ref.shape[1]
    scale = 1.0 / math.sqrt(t_ref.shape[2])
    for group in range(block // GROUP):
        rows = pl.ds(group * GROUP, GROUP)
        t_cols = [t_ref[c, rows, :].T for c in range(3)]
        c_cols = [c_ref[c, rows, :].T for c in range(3)]
        s_rows = [s_ref[c, rows, :] for c in range(3)]
        for p in range(GROUP):
            distance = None
            for c in range(3):
                apart = t_cols[c][:, p : p + 1] - s_rows[c][p : p + 1, :]
                distance = apart * apart if distance is None else distance + apart * apart
            kernel_block = 1.0 / (1.0 + distance)
            for c in range(3):
                o_ref[c, pl.ds(group * GROUP + p, 1), :] = (
                    jnp.sum(c_cols[c][:, p : p + 1] * kernel_block, axis=0, keepdims=True) * scale
                )


def pair_terms(target_shapes, source_shapes, target_cots, block=32):
    comps, pairs, points = target_shapes.shape
    spec = pl.BlockSpec((comps, block, points), lambda i: (0, i, 0))
    return pl.pallas_call(
        pair_kernel,
        grid=(pairs // block,),
        in_specs=[spec] * 3,
        out_specs=spec,
        out_shape=jax.ShapeDtypeStruct(target_shapes.shape, jnp.float32),
        name="pair_terms",
    )(target_shapes, source_shapes, target_cots)


def onehot(index, count):
    return (index[:, None] == jnp.arange(count, dtype=jnp.int32)[None, :]).astype(jnp.float32)


def on_device(
    cotangent, surface, region_id, local_target, local_shift, near_target, near_source, near_count
):
    vesicles = cotangent.shape[0]
    coef_count = cotangent.shape[2]
    devices = lax.axis_size("dev")
    slot_count = near_target.shape[2]
    pair_slots = devices * slot_count

    synthesis, quadrature, degree_scale = harmonic_tables(NLAT, NLAT)
    near_synthesis, near_quadrature, unused_scale = harmonic_tables(NEAR_LAT, NLAT)
    points = synthesis.shape[1]
    near_points = near_synthesis.shape[1]
    both = jnp.asarray(np.concatenate([synthesis, near_synthesis], axis=1).astype(np.float32))
    weights = jnp.asarray(np.concatenate([quadrature, near_quadrature]).astype(np.float32))
    contract_rows = (((0,), (0,)), ((), ()))

    cot_all = jnp.dot(
        cotangent.reshape(vesicles * 3, coef_count), both, precision=HIGHEST
    ).reshape(vesicles, 3, points + near_points)
    shape_all = jnp.dot(
        surface.reshape(vesicles * 3, coef_count), both, precision=HIGHEST
    ).reshape(vesicles, 3, points + near_points)
    cot_points = cot_all[:, :, :points]
    near_cot = cot_all[:, :, points:]
    shape_points = shape_all[:, :, :points]
    near_shape = shape_all[:, :, points:]
    stretch = 1.0 / (1.0 + jnp.sum(shape_points * shape_points, axis=1))
    point_total = stretch[:, None, :] * cot_points

    near_width = 3 * near_points
    near_rows = jnp.concatenate([near_shape, near_cot], axis=1).transpose(1, 0, 2)
    shape_rows = near_rows[:3]

    def pick(index, rows):
        return jnp.einsum("pv,kvx->kpx", onehot(index, vesicles), rows, precision=HIGHEST)

    targets = near_target[0].reshape(pair_slots)
    alive = (
        jnp.arange(slot_count, dtype=jnp.int32)[None, :] < near_count[0][:, None]
    ).reshape(pair_slots)
    picked = pick(targets, near_rows)
    kind = jnp.arange(6, dtype=jnp.int32)[:, None, None]
    picked = jnp.where((kind < 3) | alive[None, :, None], picked, 0.0)
    member = onehot(region_id, REGIONS)
    moments = cotangent[:, :, :FAR].reshape(vesicles, 3 * FAR)
    partial_far = lax.dot_general(member, moments, contract_rows, precision=HIGHEST)
    far_rows = partial_far.reshape(6, 1, slot_count, near_points)
    far_rows = jnp.broadcast_to(far_rows, (6, devices, slot_count, near_points)).reshape(
        6, pair_slots, near_points
    )
    outgoing = jnp.concatenate([picked, far_rows], axis=0)
    incoming = lax.all_to_all(outgoing, "dev", split_axis=1, concat_axis=1, tiled=True)
    far_total = jnp.sum(
        incoming[6:].reshape(6, devices, slot_count, near_points), axis=1
    ).reshape(REGIONS, 3 * FAR)
    sources = near_source[0].reshape(pair_slots)
    source_onehot = onehot(sources, vesicles)

    local_source = (local_target + local_shift) % vesicles
    local_onehot = onehot(local_source, vesicles)
    local_picked = pick(local_target, near_rows)
    local_terms = pair_terms(local_picked[:3], pick(local_source, shape_rows), local_picked[3:])
    remote_terms = pair_terms(incoming[:3], pick(sources, shape_rows), incoming[3:6])
    near_total = jnp.einsum(
        "pv,kpx->vkx", local_onehot, local_terms, precision=HIGHEST
    ) + jnp.einsum("pv,kpx->vkx", source_onehot, remote_terms, precision=HIGHEST)

    weighted = jnp.concatenate(
        [point_total, near_total.reshape(vesicles, 3, near_points)], axis=2
    ) * weights
    analysed = lax.dot_general(
        weighted.reshape(vesicles * 3, points + near_points),
        both,
        (((1,), (1,)), ((), ())),
        precision=HIGHEST,
    ).reshape(cotangent.shape)
    gradient = jnp.asarray(degree_scale.astype(np.float32)) * cotangent + analysed

    coupling = jnp.asarray(far_coupling(REGIONS, vesicles * devices).astype(np.float32))
    far_field = lax.dot_general(coupling, far_total, contract_rows, precision=HIGHEST)
    far_terms = jnp.dot(member, far_field, precision=HIGHEST).reshape(vesicles, 3, FAR)
    return gradient + jnp.pad(far_terms, ((0, 0), (0, 0), (0, coef_count - FAR)))


def solution(mesh):
    in_specs = (
        P("dev", None, None),
        P("dev", None, None),
        P("dev"),
        P("dev"),
        P("dev"),
        P("dev", None, None),
        P("dev", None, None),
        P("dev", None),
    )
    out_specs = P("dev", None, None)
    return jax.shard_map(
        on_device, mesh=mesh, in_specs=in_specs, out_specs=out_specs, check_vma=False
    )
```

```python
import math

import jax
import jax.numpy as jnp
import numpy as np
from jax import lax
from jax.experimental import pallas as pl
from jax.experimental.pallas import tpu as pltpu
from jax.sharding import PartitionSpec as P

NLAT = 24
NEAR_LAT = 8
REGIONS = 64
FAR = 8


HIGHEST = lax.Precision.HIGHEST


def harmonic_tables(grid_lat, degree_count):
    longitudes = 2 * grid_lat
    full_longitudes = 2 * degree_count
    colatitude = (np.arange(grid_lat, dtype=np.float64) + 0.5) * (math.pi / grid_lat)
    cosine = np.cos(colatitude)
    values = [np.ones_like(cosine), cosine]
    for degree in range(2, degree_count):
        values.append(((2 * degree - 1) * cosine * values[-1] - (degree - 1) * values[-2]) / degree)
    degrees = np.arange(degree_count, dtype=np.float64)
    legendre = np.stack(values[:degree_count], axis=1) * np.sqrt((2.0 * degrees + 1.0) / 2.0)
    azimuth = np.arange(longitudes, dtype=np.float64) * (2.0 * math.pi / longitudes)
    halfway = degree_count // 2
    mode_index = np.arange(degree_count, dtype=np.float64)
    frequency = np.where(mode_index < halfway, mode_index, mode_index - halfway + 1.0)
    phases = azimuth[:, None] * frequency[None, :]
    fourier = np.where(mode_index[None, :] < halfway, np.cos(phases), np.sin(phases))
    fourier = fourier * np.where(
        mode_index[None, :] == 0, math.sqrt(1.0 / full_longitudes), math.sqrt(2.0 / full_longitudes)
    )
    synthesis = np.einsum("jl,km->lmjk", legendre, fourier).reshape(
        degree_count * degree_count, grid_lat * longitudes
    )
    quadrature = np.repeat(np.sin(colatitude) * (math.pi / grid_lat), longitudes)
    degree_scale = np.repeat(1.0 / (2.0 * degrees + 1.0), degree_count)
    return (synthesis, quadrature, degree_scale)


def far_coupling(regions, vesicle_total):
    position = np.arange(regions, dtype=np.float64)
    return 1.0 / ((1.0 + np.abs(position[:, None] - position[None, :])) * math.sqrt(vesicle_total))


GROUP = 8


def pair_kernel(live_ref, t_ref, s_ref, c_ref, o_ref):
    block = t_ref.shape[1]
    first = pl.program_id(0) * block
    scale = 1.0 / math.sqrt(t_ref.shape[2])
    o_ref[...] = jnp.zeros(o_ref.shape, o_ref.dtype)
    for group in range(block // GROUP):
        rows = pl.ds(group * GROUP, GROUP)
        t_cols = [t_ref[c, rows, :].T for c in range(3)]
        c_cols = [c_ref[c, rows, :].T for c in range(3)]
        s_rows = [s_ref[c, rows, :] for c in range(3)]
        for p in range(GROUP):
            pair = group * GROUP + p

            @pl.when(live_ref[first + pair] != 0)
            def _():
                distance = None
                for c in range(3):
                    apart = t_cols[c][:, p : p + 1] - s_rows[c][p : p + 1, :]
                    distance = apart * apart if distance is None else distance + apart * apart
                kernel_block = 1.0 / (1.0 + distance)
                for c in range(3):
                    o_ref[c, pl.ds(pair, 1), :] = (
                        jnp.sum(c_cols[c][:, p : p + 1] * kernel_block, axis=0, keepdims=True)
                        * scale
                    )


def pair_terms(target_shapes, source_shapes, target_cots, block=32):
    comps, pairs, points = target_shapes.shape
    live = jnp.any(target_cots != 0.0, axis=(0, 2)).astype(jnp.int32)
    spec = pl.BlockSpec((comps, block, points), lambda i, live: (0, i, 0))
    grid_spec = pltpu.PrefetchScalarGridSpec(
        num_scalar_prefetch=1, grid=(pairs // block,), in_specs=[spec] * 3, out_specs=spec
    )
    return pl.pallas_call(
        pair_kernel,
        grid_spec=grid_spec,
        out_shape=jax.ShapeDtypeStruct(target_shapes.shape, jnp.float32),
        name="pair_terms",
    )(live, target_shapes, source_shapes, target_cots)


def onehot(index, count):
    return (index[:, None] == jnp.arange(count, dtype=jnp.int32)[None, :]).astype(jnp.float32)


def on_device(
    cotangent, surface, region_id, local_target, local_shift, near_target, near_source, near_count
):
    vesicles = cotangent.shape[0]
    coef_count = cotangent.shape[2]
    devices = lax.axis_size("dev")
    slot_count = near_target.shape[2]
    pair_slots = devices * slot_count

    synthesis, quadrature, degree_scale = harmonic_tables(NLAT, NLAT)
    near_synthesis, near_quadrature, unused_scale = harmonic_tables(NEAR_LAT, NLAT)
    points = synthesis.shape[1]
    near_points = near_synthesis.shape[1]
    both = jnp.asarray(np.concatenate([synthesis, near_synthesis], axis=1).astype(np.float32))
    weights = jnp.asarray(np.concatenate([quadrature, near_quadrature]).astype(np.float32))
    contract_rows = (((0,), (0,)), ((), ()))

    cot_all = jnp.dot(
        cotangent.reshape(vesicles * 3, coef_count), both, precision=HIGHEST
    ).reshape(vesicles, 3, points + near_points)
    shape_all = jnp.dot(
        surface.reshape(vesicles * 3, coef_count), both, precision=HIGHEST
    ).reshape(vesicles, 3, points + near_points)
    cot_points = cot_all[:, :, :points]
    near_cot = cot_all[:, :, points:]
    shape_points = shape_all[:, :, :points]
    near_shape = shape_all[:, :, points:]
    stretch = 1.0 / (1.0 + jnp.sum(shape_points * shape_points, axis=1))
    point_total = stretch[:, None, :] * cot_points

    near_width = 3 * near_points
    near_rows = jnp.concatenate([near_shape, near_cot], axis=1).transpose(1, 0, 2)
    shape_rows = near_rows[:3]

    def pick(index, rows):
        return jnp.einsum("pv,kvx->kpx", onehot(index, vesicles), rows, precision=HIGHEST)

    targets = near_target[0].reshape(pair_slots)
    alive = (
        jnp.arange(slot_count, dtype=jnp.int32)[None, :] < near_count[0][:, None]
    ).reshape(pair_slots)
    picked = pick(targets, near_rows)
    kind = jnp.arange(6, dtype=jnp.int32)[:, None, None]
    picked = jnp.where((kind < 3) | alive[None, :, None], picked, 0.0)
    member = onehot(region_id, REGIONS)
    moments = cotangent[:, :, :FAR].reshape(vesicles, 3 * FAR)
    partial_far = lax.dot_general(member, moments, contract_rows, precision=HIGHEST)
    far_rows = partial_far.reshape(6, 1, slot_count, near_points)
    far_rows = jnp.broadcast_to(far_rows, (6, devices, slot_count, near_points)).reshape(
        6, pair_slots, near_points
    )
    outgoing = jnp.concatenate([picked, far_rows], axis=0)
    incoming = lax.all_to_all(outgoing, "dev", split_axis=1, concat_axis=1, tiled=True)
    far_total = jnp.sum(
        incoming[6:].reshape(6, devices, slot_count, near_points), axis=1
    ).reshape(REGIONS, 3 * FAR)
    sources = near_source[0].reshape(pair_slots)
    source_onehot = onehot(sources, vesicles)

    local_source = (local_target + local_shift) % vesicles
    local_onehot = onehot(local_source, vesicles)
    local_picked = pick(local_target, near_rows)
    local_terms = pair_terms(local_picked[:3], pick(local_source, shape_rows), local_picked[3:])
    remote_terms = pair_terms(incoming[:3], pick(sources, shape_rows), incoming[3:6])
    near_total = jnp.einsum(
        "pv,kpx->vkx", local_onehot, local_terms, precision=HIGHEST
    ) + jnp.einsum("pv,kpx->vkx", source_onehot, remote_terms, precision=HIGHEST)

    weighted = jnp.concatenate(
        [point_total, near_total.reshape(vesicles, 3, near_points)], axis=2
    ) * weights
    analysed = lax.dot_general(
        weighted.reshape(vesicles * 3, points + near_points),
        both,
        (((1,), (1,)), ((), ())),
        precision=HIGHEST,
    ).reshape(cotangent.shape)
    gradient = jnp.asarray(degree_scale.astype(np.float32)) * cotangent + analysed

    coupling = jnp.asarray(far_coupling(REGIONS, vesicles * devices).astype(np.float32))
    far_field = lax.dot_general(coupling, far_total, contract_rows, precision=HIGHEST)
    far_terms = jnp.dot(member, far_field, precision=HIGHEST).reshape(vesicles, 3, FAR)
    return gradient + jnp.pad(far_terms, ((0, 0), (0, 0), (0, coef_count - FAR)))


def solution(mesh):
    in_specs = (
        P("dev", None, None),
        P("dev", None, None),
        P("dev"),
        P("dev"),
        P("dev"),
        P("dev", None, None),
        P("dev", None, None),
        P("dev", None),
    )
    out_specs = P("dev", None, None)
    return jax.shard_map(
        on_device, mesh=mesh, in_specs=in_specs, out_specs=out_specs, check_vma=False
    )
```

```python
import math

import jax
import jax.numpy as jnp
import numpy as np
from jax import lax
from jax.experimental import pallas as pl
from jax.experimental.pallas import tpu as pltpu
from jax.sharding import PartitionSpec as P

NLAT = 24
NEAR_LAT = 8
REGIONS = 64
FAR = 8


HIGHEST = lax.Precision.HIGHEST


def harmonic_tables(grid_lat, degree_count):
    longitudes = 2 * grid_lat
    full_longitudes = 2 * degree_count
    colatitude = (np.arange(grid_lat, dtype=np.float64) + 0.5) * (math.pi / grid_lat)
    cosine = np.cos(colatitude)
    values = [np.ones_like(cosine), cosine]
    for degree in range(2, degree_count):
        values.append(((2 * degree - 1) * cosine * values[-1] - (degree - 1) * values[-2]) / degree)
    degrees = np.arange(degree_count, dtype=np.float64)
    legendre = np.stack(values[:degree_count], axis=1) * np.sqrt((2.0 * degrees + 1.0) / 2.0)
    azimuth = np.arange(longitudes, dtype=np.float64) * (2.0 * math.pi / longitudes)
    halfway = degree_count // 2
    mode_index = np.arange(degree_count, dtype=np.float64)
    frequency = np.where(mode_index < halfway, mode_index, mode_index - halfway + 1.0)
    phases = azimuth[:, None] * frequency[None, :]
    fourier = np.where(mode_index[None, :] < halfway, np.cos(phases), np.sin(phases))
    fourier = fourier * np.where(
        mode_index[None, :] == 0, math.sqrt(1.0 / full_longitudes), math.sqrt(2.0 / full_longitudes)
    )
    synthesis = np.einsum("jl,km->lmjk", legendre, fourier).reshape(
        degree_count * degree_count, grid_lat * longitudes
    )
    quadrature = np.repeat(np.sin(colatitude) * (math.pi / grid_lat), longitudes)
    degree_scale = np.repeat(1.0 / (2.0 * degrees + 1.0), degree_count)
    return (synthesis, quadrature, degree_scale)


def far_coupling(regions, vesicle_total):
    position = np.arange(regions, dtype=np.float64)
    return 1.0 / ((1.0 + np.abs(position[:, None] - position[None, :])) * math.sqrt(vesicle_total))


GROUP = 8


def pair_kernel(count_ref, t_ref, s_ref, c_ref, o_ref):
    block = t_ref.shape[1]
    scale = 1.0 / math.sqrt(t_ref.shape[2])
    busy = pl.program_id(0) * block < count_ref[0]

    @pl.when(busy)
    def _():
        for group in range(block // GROUP):
            rows = pl.ds(group * GROUP, GROUP)
            t_cols = [t_ref[c, rows, :].T for c in range(3)]
            c_cols = [c_ref[c, rows, :].T for c in range(3)]
            s_rows = [s_ref[c, rows, :] for c in range(3)]
            for p in range(GROUP):
                distance = None
                for c in range(3):
                    apart = t_cols[c][:, p : p + 1] - s_rows[c][p : p + 1, :]
                    distance = apart * apart if distance is None else distance + apart * apart
                kernel_block = 1.0 / (1.0 + distance)
                for c in range(3):
                    o_ref[c, pl.ds(group * GROUP + p, 1), :] = (
                        jnp.sum(c_cols[c][:, p : p + 1] * kernel_block, axis=0, keepdims=True)
                        * scale
                    )

    @pl.when(jnp.logical_not(busy))
    def _():
        o_ref[...] = jnp.zeros(o_ref.shape, o_ref.dtype)


def pair_terms(target_shapes, source_shapes, target_cots, count, block=32):
    comps, pairs, points = target_shapes.shape
    spec = pl.BlockSpec((comps, block, points), lambda i, count: (0, i, 0))
    grid_spec = pltpu.PrefetchScalarGridSpec(
        num_scalar_prefetch=1, grid=(pairs // block,), in_specs=[spec] * 3, out_specs=spec
    )
    return pl.pallas_call(
        pair_kernel,
        grid_spec=grid_spec,
        out_shape=jax.ShapeDtypeStruct(target_shapes.shape, jnp.float32),
        name="pair_terms",
    )(count.reshape(1), target_shapes, source_shapes, target_cots)


def onehot(index, count):
    return (index[:, None] == jnp.arange(count, dtype=jnp.int32)[None, :]).astype(jnp.float32)


def on_device(
    cotangent, surface, region_id, local_target, local_shift, near_target, near_source, near_count
):
    vesicles = cotangent.shape[0]
    coef_count = cotangent.shape[2]
    devices = lax.axis_size("dev")
    slot_count = near_target.shape[2]
    pair_slots = devices * slot_count

    synthesis, quadrature, degree_scale = harmonic_tables(NLAT, NLAT)
    near_synthesis, near_quadrature, unused_scale = harmonic_tables(NEAR_LAT, NLAT)
    points = synthesis.shape[1]
    near_points = near_synthesis.shape[1]
    both = jnp.asarray(np.concatenate([synthesis, near_synthesis], axis=1).astype(np.float32))
    weights = jnp.asarray(np.concatenate([quadrature, near_quadrature]).astype(np.float32))
    contract_rows = (((0,), (0,)), ((), ()))

    cot_all = jnp.dot(
        cotangent.reshape(vesicles * 3, coef_count), both, precision=HIGHEST
    ).reshape(vesicles, 3, points + near_points)
    shape_all = jnp.dot(
        surface.reshape(vesicles * 3, coef_count), both, precision=HIGHEST
    ).reshape(vesicles, 3, points + near_points)
    cot_points = cot_all[:, :, :points]
    near_cot = cot_all[:, :, points:]
    shape_points = shape_all[:, :, :points]
    near_shape = shape_all[:, :, points:]
    stretch = 1.0 / (1.0 + jnp.sum(shape_points * shape_points, axis=1))
    point_total = stretch[:, None, :] * cot_points

    near_width = 3 * near_points
    near_rows = jnp.concatenate([near_shape, near_cot], axis=1).transpose(1, 0, 2)
    shape_rows = near_rows[:3]

    def pick(index, rows):
        return jnp.einsum("pv,kvx->kpx", onehot(index, vesicles), rows, precision=HIGHEST)

    targets = near_target[0].reshape(pair_slots)
    alive = (
        jnp.arange(slot_count, dtype=jnp.int32)[None, :] < near_count[0][:, None]
    ).reshape(pair_slots)
    picked = pick(targets, near_rows)
    kind = jnp.arange(6, dtype=jnp.int32)[:, None, None]
    picked = jnp.where((kind < 3) | alive[None, :, None], picked, 0.0)
    member = onehot(region_id, REGIONS)
    moments = cotangent[:, :, :FAR].reshape(vesicles, 3 * FAR)
    partial_far = lax.dot_general(member, moments, contract_rows, precision=HIGHEST)
    far_rows = partial_far.reshape(6, 1, slot_count, near_points)
    far_rows = jnp.broadcast_to(far_rows, (6, devices, slot_count, near_points)).reshape(
        6, pair_slots, near_points
    )
    outgoing = jnp.concatenate([picked, far_rows], axis=0)
    incoming = lax.all_to_all(outgoing, "dev", split_axis=1, concat_axis=1, tiled=True)
    far_total = jnp.sum(
        incoming[6:].reshape(6, devices, slot_count, near_points), axis=1
    ).reshape(REGIONS, 3 * FAR)
    sources = near_source[0].reshape(pair_slots)
    live = jnp.any(incoming[3:6] != 0.0, axis=(0, 2)).astype(jnp.int32)
    live_count = jnp.sum(live)
    position = jnp.where(
        live != 0, jnp.cumsum(live) - 1, live_count + jnp.cumsum(1 - live) - 1
    )
    order = onehot(position, pair_slots).T
    packed = jnp.einsum("np,kpx->knx", order, incoming[:6], precision=HIGHEST)
    source_onehot = jnp.dot(order, onehot(sources, vesicles), precision=HIGHEST)

    local_source = (local_target + local_shift) % vesicles
    local_onehot = onehot(local_source, vesicles)
    local_picked = pick(local_target, near_rows)
    local_terms = pair_terms(
        local_picked[:3],
        pick(local_source, shape_rows),
        local_picked[3:],
        jnp.full((), vesicles, jnp.int32),
    )
    remote_terms = pair_terms(
        packed[:3],
        jnp.einsum("pv,kvx->kpx", source_onehot, shape_rows, precision=HIGHEST),
        packed[3:],
        live_count,
    )
    near_total = jnp.einsum(
        "pv,kpx->vkx", local_onehot, local_terms, precision=HIGHEST
    ) + jnp.einsum("pv,kpx->vkx", source_onehot, remote_terms, precision=HIGHEST)

    weighted = jnp.concatenate(
        [point_total, near_total.reshape(vesicles, 3, near_points)], axis=2
    ) * weights
    analysed = lax.dot_general(
        weighted.reshape(vesicles * 3, points + near_points),
        both,
        (((1,), (1,)), ((), ())),
        precision=HIGHEST,
    ).reshape(cotangent.shape)
    gradient = jnp.asarray(degree_scale.astype(np.float32)) * cotangent + analysed

    coupling = jnp.asarray(far_coupling(REGIONS, vesicles * devices).astype(np.float32))
    far_field = lax.dot_general(coupling, far_total, contract_rows, precision=HIGHEST)
    far_terms = jnp.dot(member, far_field, precision=HIGHEST).reshape(vesicles, 3, FAR)
    return gradient + jnp.pad(far_terms, ((0, 0), (0, 0), (0, coef_count - FAR)))


def solution(mesh):
    in_specs = (
        P("dev", None, None),
        P("dev", None, None),
        P("dev"),
        P("dev"),
        P("dev"),
        P("dev", None, None),
        P("dev", None, None),
        P("dev", None),
    )
    out_specs = P("dev", None, None)
    return jax.shard_map(
        on_device, mesh=mesh, in_specs=in_specs, out_specs=out_specs, check_vma=False
    )
```

```python
import math

import jax
import jax.numpy as jnp
import numpy as np
from jax import lax
from jax.sharding import PartitionSpec as P

NLAT = 24
NEAR_LAT = 8
REGIONS = 64
FAR = 8


HIGHEST = lax.Precision.HIGHEST


def harmonic_tables(grid_lat, degree_count):
    longitudes = 2 * grid_lat
    full_longitudes = 2 * degree_count
    colatitude = (np.arange(grid_lat, dtype=np.float64) + 0.5) * (math.pi / grid_lat)
    cosine = np.cos(colatitude)
    values = [np.ones_like(cosine), cosine]
    for degree in range(2, degree_count):
        values.append(((2 * degree - 1) * cosine * values[-1] - (degree - 1) * values[-2]) / degree)
    degrees = np.arange(degree_count, dtype=np.float64)
    legendre = np.stack(values[:degree_count], axis=1) * np.sqrt((2.0 * degrees + 1.0) / 2.0)
    azimuth = np.arange(longitudes, dtype=np.float64) * (2.0 * math.pi / longitudes)
    halfway = degree_count // 2
    mode_index = np.arange(degree_count, dtype=np.float64)
    frequency = np.where(mode_index < halfway, mode_index, mode_index - halfway + 1.0)
    phases = azimuth[:, None] * frequency[None, :]
    fourier = np.where(mode_index[None, :] < halfway, np.cos(phases), np.sin(phases))
    fourier = fourier * np.where(
        mode_index[None, :] == 0, math.sqrt(1.0 / full_longitudes), math.sqrt(2.0 / full_longitudes)
    )
    synthesis = np.einsum("jl,km->lmjk", legendre, fourier).reshape(
        degree_count * degree_count, grid_lat * longitudes
    )
    quadrature = np.repeat(np.sin(colatitude) * (math.pi / grid_lat), longitudes)
    degree_scale = np.repeat(1.0 / (2.0 * degrees + 1.0), degree_count)
    return (synthesis, quadrature, degree_scale)


def far_coupling(regions, vesicle_total):
    position = np.arange(regions, dtype=np.float64)
    return 1.0 / ((1.0 + np.abs(position[:, None] - position[None, :])) * math.sqrt(vesicle_total))


def pair_terms(target_shapes, source_shapes, target_cots):
    distance = jnp.zeros(
        (target_shapes.shape[1], target_shapes.shape[2], source_shapes.shape[2]), jnp.float32
    )
    for component in range(3):
        apart = target_shapes[component, :, :, None] - source_shapes[component, :, None, :]
        distance = distance + apart * apart
    kernel_block = 1.0 / (1.0 + distance)
    scale = 1.0 / math.sqrt(target_shapes.shape[2])
    return jnp.einsum("cpa,pab->cpb", target_cots, kernel_block, precision=HIGHEST) * scale


def onehot(index, count):
    return (index[:, None] == jnp.arange(count, dtype=jnp.int32)[None, :]).astype(jnp.float32)


def on_device(
    cotangent, surface, region_id, local_target, local_shift, near_target, near_source, near_count
):
    vesicles = cotangent.shape[0]
    coef_count = cotangent.shape[2]
    devices = lax.axis_size("dev")
    slot_count = near_target.shape[2]
    pair_slots = devices * slot_count

    synthesis, quadrature, degree_scale = harmonic_tables(NLAT, NLAT)
    near_synthesis, near_quadrature, unused_scale = harmonic_tables(NEAR_LAT, NLAT)
    points = synthesis.shape[1]
    near_points = near_synthesis.shape[1]
    full = jnp.asarray(synthesis.astype(np.float32))
    near = jnp.asarray(near_synthesis.astype(np.float32))
    contract_rows = (((0,), (0,)), ((), ()))
    cot_flat = cotangent.reshape(vesicles * 3, coef_count)
    surface_flat = surface.reshape(vesicles * 3, coef_count)

    near_cot = jnp.dot(cot_flat, near, precision=HIGHEST).reshape(vesicles, 3, near_points)
    near_shape = jnp.dot(surface_flat, near, precision=HIGHEST).reshape(vesicles, 3, near_points)
    cot_points = jnp.dot(cot_flat, full, precision=HIGHEST).reshape(vesicles, 3, points)
    shape_points = jnp.dot(surface_flat, full, precision=HIGHEST).reshape(vesicles, 3, points)
    stretch = 1.0 / (1.0 + jnp.sum(shape_points * shape_points, axis=1))
    point_total = stretch[:, None, :] * cot_points * jnp.asarray(quadrature.astype(np.float32))
    contract_points = (((1,), (1,)), ((), ()))
    point_coefs = lax.dot_general(
        point_total.reshape(vesicles * 3, points), full, contract_points, precision=HIGHEST
    )
    gradient = jnp.asarray(degree_scale.astype(np.float32)) * cotangent + point_coefs.reshape(
        cotangent.shape
    )

    near_width = 3 * near_points
    near_rows = jnp.concatenate([near_shape, near_cot], axis=1).transpose(1, 0, 2)
    shape_rows = near_rows[:3]

    def pick(index, rows):
        return jnp.einsum("pv,kvx->kpx", onehot(index, vesicles), rows, precision=HIGHEST)

    targets = near_target[0].reshape(pair_slots)
    alive = (
        jnp.arange(slot_count, dtype=jnp.int32)[None, :] < near_count[0][:, None]
    ).reshape(pair_slots)
    picked = pick(targets, near_rows)
    kind = jnp.arange(6, dtype=jnp.int32)[:, None, None]
    picked = jnp.where((kind < 3) | alive[None, :, None], picked, 0.0)
    member = onehot(region_id, REGIONS)
    moments = cotangent[:, :, :FAR].reshape(vesicles, 3 * FAR)
    partial_far = lax.dot_general(member, moments, contract_rows, precision=HIGHEST)
    far_rows = partial_far.reshape(6, 1, slot_count, near_points)
    far_rows = jnp.broadcast_to(far_rows, (6, devices, slot_count, near_points)).reshape(
        6, pair_slots, near_points
    )
    outgoing = jnp.concatenate([picked, far_rows], axis=0)
    incoming = lax.all_to_all(outgoing, "dev", split_axis=1, concat_axis=1, tiled=True)
    far_total = jnp.sum(
        incoming[6:].reshape(6, devices, slot_count, near_points), axis=1
    ).reshape(REGIONS, 3 * FAR)
    sources = near_source[0].reshape(pair_slots)
    source_onehot = onehot(sources, vesicles)

    local_source = (local_target + local_shift) % vesicles
    local_onehot = onehot(local_source, vesicles)
    local_picked = pick(local_target, near_rows)
    local_terms = pair_terms(local_picked[:3], pick(local_source, shape_rows), local_picked[3:])
    remote_terms = pair_terms(incoming[:3], pick(sources, shape_rows), incoming[3:6])
    near_total = jnp.einsum(
        "pv,kpx->vkx", local_onehot, local_terms, precision=HIGHEST
    ) + jnp.einsum("pv,kpx->vkx", source_onehot, remote_terms, precision=HIGHEST)

    near_weighted = near_total.reshape(vesicles * 3, near_points) * jnp.asarray(
        near_quadrature.astype(np.float32)
    )
    gradient = gradient + lax.dot_general(
        near_weighted, near, contract_points, precision=HIGHEST
    ).reshape(cotangent.shape)

    coupling = jnp.asarray(far_coupling(REGIONS, vesicles * devices).astype(np.float32))
    far_field = lax.dot_general(coupling, far_total, contract_rows, precision=HIGHEST)
    far_terms = jnp.dot(member, far_field, precision=HIGHEST).reshape(vesicles, 3, FAR)
    return gradient + jnp.pad(far_terms, ((0, 0), (0, 0), (0, coef_count - FAR)))


def solution(mesh):
    in_specs = (
        P("dev", None, None),
        P("dev", None, None),
        P("dev"),
        P("dev"),
        P("dev"),
        P("dev", None, None),
        P("dev", None, None),
        P("dev", None),
    )
    out_specs = P("dev", None, None)
    return jax.shard_map(
        on_device, mesh=mesh, in_specs=in_specs, out_specs=out_specs, check_vma=False
    )
```

```python
import math

import jax
import jax.numpy as jnp
import numpy as np
from jax import lax
from jax.sharding import PartitionSpec as P

NLAT = 24
NEAR_LAT = 8
REGIONS = 64
FAR = 8


HIGHEST = lax.Precision.HIGHEST


def harmonic_tables(grid_lat, degree_count):
    longitudes = 2 * grid_lat
    full_longitudes = 2 * degree_count
    colatitude = (np.arange(grid_lat, dtype=np.float64) + 0.5) * (math.pi / grid_lat)
    cosine = np.cos(colatitude)
    values = [np.ones_like(cosine), cosine]
    for degree in range(2, degree_count):
        values.append(((2 * degree - 1) * cosine * values[-1] - (degree - 1) * values[-2]) / degree)
    degrees = np.arange(degree_count, dtype=np.float64)
    legendre = np.stack(values[:degree_count], axis=1) * np.sqrt((2.0 * degrees + 1.0) / 2.0)
    azimuth = np.arange(longitudes, dtype=np.float64) * (2.0 * math.pi / longitudes)
    halfway = degree_count // 2
    mode_index = np.arange(degree_count, dtype=np.float64)
    frequency = np.where(mode_index < halfway, mode_index, mode_index - halfway + 1.0)
    phases = azimuth[:, None] * frequency[None, :]
    fourier = np.where(mode_index[None, :] < halfway, np.cos(phases), np.sin(phases))
    fourier = fourier * np.where(
        mode_index[None, :] == 0, math.sqrt(1.0 / full_longitudes), math.sqrt(2.0 / full_longitudes)
    )
    synthesis = np.einsum("jl,km->lmjk", legendre, fourier).reshape(
        degree_count * degree_count, grid_lat * longitudes
    )
    quadrature = np.repeat(np.sin(colatitude) * (math.pi / grid_lat), longitudes)
    degree_scale = np.repeat(1.0 / (2.0 * degrees + 1.0), degree_count)
    return (synthesis, quadrature, degree_scale)


def far_coupling(regions, vesicle_total):
    position = np.arange(regions, dtype=np.float64)
    return 1.0 / ((1.0 + np.abs(position[:, None] - position[None, :])) * math.sqrt(vesicle_total))


def pair_terms(target_shapes, source_shapes, target_cots):
    distance = jnp.zeros(
        (target_shapes.shape[1], target_shapes.shape[2], source_shapes.shape[2]), jnp.float32
    )
    for component in range(3):
        apart = target_shapes[component, :, :, None] - source_shapes[component, :, None, :]
        distance = distance + apart * apart
    kernel_block = 1.0 / (1.0 + distance)
    scale = 1.0 / math.sqrt(target_shapes.shape[2])
    return jnp.einsum("cpa,pab->cpb", target_cots, kernel_block, precision=HIGHEST) * scale


def onehot(index, count):
    return (index[:, None] == jnp.arange(count, dtype=jnp.int32)[None, :]).astype(jnp.float32)


def on_device(
    cotangent, surface, region_id, local_target, local_shift, near_target, near_source, near_count
):
    vesicles = cotangent.shape[0]
    coef_count = cotangent.shape[2]
    devices = lax.axis_size("dev")
    slot_count = near_target.shape[2]
    pair_slots = devices * slot_count

    synthesis, quadrature, degree_scale = harmonic_tables(NLAT, NLAT)
    near_synthesis, near_quadrature, unused_scale = harmonic_tables(NEAR_LAT, NLAT)
    points = synthesis.shape[1]
    near_points = near_synthesis.shape[1]
    full = jnp.asarray(synthesis.astype(np.float32))
    near = jnp.asarray(near_synthesis.astype(np.float32))
    contract_rows = (((0,), (0,)), ((), ()))
    cot_flat = cotangent.reshape(vesicles * 3, coef_count)
    surface_flat = surface.reshape(vesicles * 3, coef_count)

    near_cot = jnp.dot(cot_flat, near, precision=HIGHEST).reshape(vesicles, 3, near_points)
    near_shape = jnp.dot(surface_flat, near, precision=HIGHEST).reshape(vesicles, 3, near_points)
    cot_points = jnp.dot(cot_flat, full, precision=HIGHEST).reshape(vesicles, 3, points)
    shape_points = jnp.dot(surface_flat, full, precision=HIGHEST).reshape(vesicles, 3, points)
    stretch = 1.0 / (1.0 + jnp.sum(shape_points * shape_points, axis=1))
    point_total = stretch[:, None, :] * cot_points * jnp.asarray(quadrature.astype(np.float32))
    contract_points = (((1,), (1,)), ((), ()))
    point_coefs = lax.dot_general(
        point_total.reshape(vesicles * 3, points), full, contract_points, precision=HIGHEST
    )
    gradient = lax.optimization_barrier(
        jnp.asarray(degree_scale.astype(np.float32)) * cotangent
        + point_coefs.reshape(cotangent.shape)
    )

    near_width = 3 * near_points
    near_rows = jnp.concatenate([near_shape, near_cot], axis=1).transpose(1, 0, 2)
    shape_rows = near_rows[:3]

    def pick(index, rows):
        return jnp.einsum("pv,kvx->kpx", onehot(index, vesicles), rows, precision=HIGHEST)

    targets = near_target[0].reshape(pair_slots)
    alive = (
        jnp.arange(slot_count, dtype=jnp.int32)[None, :] < near_count[0][:, None]
    ).reshape(pair_slots)
    picked = pick(targets, near_rows)
    kind = jnp.arange(6, dtype=jnp.int32)[:, None, None]
    picked = jnp.where((kind < 3) | alive[None, :, None], picked, 0.0)
    member = onehot(region_id, REGIONS)
    moments = cotangent[:, :, :FAR].reshape(vesicles, 3 * FAR)
    partial_far = lax.dot_general(member, moments, contract_rows, precision=HIGHEST)
    far_rows = partial_far.reshape(6, 1, slot_count, near_points)
    far_rows = jnp.broadcast_to(far_rows, (6, devices, slot_count, near_points)).reshape(
        6, pair_slots, near_points
    )
    outgoing = jnp.concatenate([picked, far_rows], axis=0)
    incoming = lax.all_to_all(outgoing, "dev", split_axis=1, concat_axis=1, tiled=True)
    slot_of = onehot(jnp.arange(pair_slots, dtype=jnp.int32) % slot_count, slot_count)
    far_total = jnp.einsum(
        "kpx,ps->ksx", incoming[6:], slot_of, precision=HIGHEST
    ).reshape(REGIONS, 3 * FAR)
    sources = near_source[0].reshape(pair_slots)
    source_onehot = onehot(sources, vesicles)

    local_source = (local_target + local_shift) % vesicles
    local_onehot = onehot(local_source, vesicles)
    local_picked = pick(local_target, near_rows)
    local_terms = pair_terms(local_picked[:3], pick(local_source, shape_rows), local_picked[3:])
    remote_terms = pair_terms(incoming[:3], pick(sources, shape_rows), incoming[3:6])
    near_total = jnp.einsum(
        "pv,kpx->vkx", local_onehot, local_terms, precision=HIGHEST
    ) + jnp.einsum("pv,kpx->vkx", source_onehot, remote_terms, precision=HIGHEST)

    near_weighted = near_total.reshape(vesicles * 3, near_points) * jnp.asarray(
        near_quadrature.astype(np.float32)
    )
    gradient = gradient + lax.dot_general(
        near_weighted, near, contract_points, precision=HIGHEST
    ).reshape(cotangent.shape)

    coupling = jnp.asarray(far_coupling(REGIONS, vesicles * devices).astype(np.float32))
    far_field = lax.dot_general(coupling, far_total, contract_rows, precision=HIGHEST)
    far_terms = jnp.dot(member, far_field, precision=HIGHEST).reshape(vesicles, 3, FAR)
    return gradient + jnp.pad(far_terms, ((0, 0), (0, 0), (0, coef_count - FAR)))


def solution(mesh):
    in_specs = (
        P("dev", None, None),
        P("dev", None, None),
        P("dev"),
        P("dev"),
        P("dev"),
        P("dev", None, None),
        P("dev", None, None),
        P("dev", None),
    )
    out_specs = P("dev", None, None)
    return jax.shard_map(
        on_device, mesh=mesh, in_specs=in_specs, out_specs=out_specs, check_vma=False
    )
```

```python
import math

import jax
import jax.numpy as jnp
import numpy as np
from jax import lax
from jax.experimental import pallas as pl
from jax.experimental.pallas import tpu as pltpu
from jax.sharding import PartitionSpec as P

NLAT = 24
NEAR_LAT = 8
REGIONS = 64
FAR = 8


HIGHEST = lax.Precision.HIGHEST


def harmonic_tables(grid_lat, degree_count):
    longitudes = 2 * grid_lat
    full_longitudes = 2 * degree_count
    colatitude = (np.arange(grid_lat, dtype=np.float64) + 0.5) * (math.pi / grid_lat)
    cosine = np.cos(colatitude)
    values = [np.ones_like(cosine), cosine]
    for degree in range(2, degree_count):
        values.append(((2 * degree - 1) * cosine * values[-1] - (degree - 1) * values[-2]) / degree)
    degrees = np.arange(degree_count, dtype=np.float64)
    legendre = np.stack(values[:degree_count], axis=1) * np.sqrt((2.0 * degrees + 1.0) / 2.0)
    azimuth = np.arange(longitudes, dtype=np.float64) * (2.0 * math.pi / longitudes)
    halfway = degree_count // 2
    mode_index = np.arange(degree_count, dtype=np.float64)
    frequency = np.where(mode_index < halfway, mode_index, mode_index - halfway + 1.0)
    phases = azimuth[:, None] * frequency[None, :]
    fourier = np.where(mode_index[None, :] < halfway, np.cos(phases), np.sin(phases))
    fourier = fourier * np.where(
        mode_index[None, :] == 0, math.sqrt(1.0 / full_longitudes), math.sqrt(2.0 / full_longitudes)
    )
    synthesis = np.einsum("jl,km->lmjk", legendre, fourier).reshape(
        degree_count * degree_count, grid_lat * longitudes
    )
    quadrature = np.repeat(np.sin(colatitude) * (math.pi / grid_lat), longitudes)
    degree_scale = np.repeat(1.0 / (2.0 * degrees + 1.0), degree_count)
    return (synthesis, quadrature, degree_scale)


def far_coupling(regions, vesicle_total):
    position = np.arange(regions, dtype=np.float64)
    return 1.0 / ((1.0 + np.abs(position[:, None] - position[None, :])) * math.sqrt(vesicle_total))


GROUP = 8

def gather_pair_kernel(live_ref, tidx_ref, sidx_ref, t_ref, s_ref, o_ref, order_ref, tile_ref):
    pairs = live_ref.shape[0]
    scale = 1.0 / math.sqrt(t_ref.shape[2])
    o_ref[...] = jnp.zeros(o_ref.shape, o_ref.dtype)

    def pack(p, count):
        order_ref[count] = p
        return count + live_ref[p]

    count = lax.fori_loop(0, pairs, pack, 0, unroll=8)
    for j in range(GROUP):
        order_ref[count + j] = order_ref[0]

    def group_body(g, carry):
        picked = [order_ref[g * GROUP + j] for j in range(GROUP)]
        for j in range(GROUP):
            t_row = tidx_ref[picked[j]]
            s_row = sidx_ref[picked[j]]
            for k in range(6):
                tile_ref[k, pl.ds(j, 1), :] = t_ref[k, pl.ds(t_row, 1), :]
            for c in range(3):
                tile_ref[6 + c, pl.ds(j, 1), :] = s_ref[c, pl.ds(s_row, 1), :]
        t_cols = [tile_ref[c].T for c in range(3)]
        c_cols = [tile_ref[3 + c].T for c in range(3)]
        s_rows = [tile_ref[6 + c] for c in range(3)]
        for p in range(GROUP):
            distance = None
            for c in range(3):
                apart = t_cols[c][:, p : p + 1] - s_rows[c][p : p + 1, :]
                distance = apart * apart if distance is None else distance + apart * apart
            kernel_block = 1.0 / (1.0 + distance)
            for c in range(3):
                o_ref[c, pl.ds(picked[p], 1), :] = (
                    jnp.sum(c_cols[c][:, p : p + 1] * kernel_block, axis=0, keepdims=True) * scale
                )
        return carry

    lax.fori_loop(0, (count + GROUP - 1) // GROUP, group_body, 0)


def gather_pair_terms(live, target_index, source_index, target_rows, source_rows):
    pairs = live.shape[0]
    points = target_rows.shape[2]
    vmem = pl.BlockSpec(memory_space=pltpu.VMEM)
    smem = pl.BlockSpec(memory_space=pltpu.SMEM)
    return pl.pallas_call(
        gather_pair_kernel,
        in_specs=[smem, smem, smem, vmem, vmem],
        out_specs=vmem,
        out_shape=jax.ShapeDtypeStruct((3, pairs, points), jnp.float32),
        scratch_shapes=[pltpu.SMEM((pairs + GROUP,), jnp.int32), pltpu.VMEM((9, GROUP, points), jnp.float32)],
        name="gather_pair_terms",
    )(live, target_index, source_index, target_rows, source_rows)

def onehot(index, count):
    return (index[:, None] == jnp.arange(count, dtype=jnp.int32)[None, :]).astype(jnp.float32)


def on_device(
    cotangent, surface, region_id, local_target, local_shift, near_target, near_source, near_count
):
    vesicles = cotangent.shape[0]
    coef_count = cotangent.shape[2]
    devices = lax.axis_size("dev")
    slot_count = near_target.shape[2]
    pair_slots = devices * slot_count

    synthesis, quadrature, degree_scale = harmonic_tables(NLAT, NLAT)
    near_synthesis, near_quadrature, unused_scale = harmonic_tables(NEAR_LAT, NLAT)
    points = synthesis.shape[1]
    near_points = near_synthesis.shape[1]
    full = jnp.asarray(synthesis.astype(np.float32))
    near = jnp.asarray(near_synthesis.astype(np.float32))
    contract_rows = (((0,), (0,)), ((), ()))
    cot_flat = cotangent.reshape(vesicles * 3, coef_count)
    surface_flat = surface.reshape(vesicles * 3, coef_count)

    near_cot = jnp.dot(cot_flat, near, precision=HIGHEST).reshape(vesicles, 3, near_points)
    near_shape = jnp.dot(surface_flat, near, precision=HIGHEST).reshape(vesicles, 3, near_points)
    cot_points = jnp.dot(cot_flat, full, precision=HIGHEST).reshape(vesicles, 3, points)
    shape_points = jnp.dot(surface_flat, full, precision=HIGHEST).reshape(vesicles, 3, points)
    stretch = 1.0 / (1.0 + jnp.sum(shape_points * shape_points, axis=1))
    point_total = stretch[:, None, :] * cot_points * jnp.asarray(quadrature.astype(np.float32))
    contract_points = (((1,), (1,)), ((), ()))
    point_coefs = lax.dot_general(
        point_total.reshape(vesicles * 3, points), full, contract_points, precision=HIGHEST
    )
    gradient = lax.optimization_barrier(
        jnp.asarray(degree_scale.astype(np.float32)) * cotangent
        + point_coefs.reshape(cotangent.shape)
    )

    near_width = 3 * near_points
    near_rows = jnp.concatenate([near_shape, near_cot], axis=1).transpose(1, 0, 2)
    shape_rows = near_rows[:3]

    def pick(index, rows):
        return jnp.einsum("pv,kvx->kpx", onehot(index, vesicles), rows, precision=HIGHEST)

    targets = near_target[0].reshape(pair_slots)
    alive = (
        jnp.arange(slot_count, dtype=jnp.int32)[None, :] < near_count[0][:, None]
    ).reshape(pair_slots)
    picked = pick(targets, near_rows)
    kind = jnp.arange(6, dtype=jnp.int32)[:, None, None]
    picked = jnp.where((kind < 3) | alive[None, :, None], picked, 0.0)
    member = onehot(region_id, REGIONS)
    moments = cotangent[:, :, :FAR].reshape(vesicles, 3 * FAR)
    partial_far = lax.dot_general(member, moments, contract_rows, precision=HIGHEST)
    far_rows = partial_far.reshape(6, 1, slot_count, near_points)
    far_rows = jnp.broadcast_to(far_rows, (6, devices, slot_count, near_points)).reshape(
        6, pair_slots, near_points
    )
    outgoing = jnp.concatenate([picked, far_rows], axis=0)
    incoming = lax.all_to_all(outgoing, "dev", split_axis=1, concat_axis=1, tiled=True)
    slot_of = onehot(jnp.arange(pair_slots, dtype=jnp.int32) % slot_count, slot_count)
    far_total = jnp.einsum(
        "kpx,ps->ksx", incoming[6:], slot_of, precision=HIGHEST
    ).reshape(REGIONS, 3 * FAR)
    sources = jnp.clip(near_source[0].reshape(pair_slots), 0, vesicles - 1)
    source_onehot = onehot(sources, vesicles)

    local_target = jnp.clip(local_target, 0, vesicles - 1)
    local_source = (local_target + local_shift) % vesicles
    local_onehot = onehot(local_source, vesicles)
    local_terms = gather_pair_terms(
        jnp.ones((vesicles,), jnp.int32), local_target, local_source, near_rows, shape_rows
    )
    live = jnp.any(incoming[3:6] != 0.0, axis=(0, 2)).astype(jnp.int32)
    remote_terms = gather_pair_terms(
        live, jnp.arange(pair_slots, dtype=jnp.int32), sources, incoming, shape_rows
    )
    near_total = jnp.einsum(
        "pv,kpx->vkx", local_onehot, local_terms, precision=HIGHEST
    ) + jnp.einsum("pv,kpx->vkx", source_onehot, remote_terms, precision=HIGHEST)

    near_weighted = near_total.reshape(vesicles * 3, near_points) * jnp.asarray(
        near_quadrature.astype(np.float32)
    )
    gradient = gradient + lax.dot_general(
        near_weighted, near, contract_points, precision=HIGHEST
    ).reshape(cotangent.shape)

    coupling = jnp.asarray(far_coupling(REGIONS, vesicles * devices).astype(np.float32))
    far_field = lax.dot_general(coupling, far_total, contract_rows, precision=HIGHEST)
    far_terms = jnp.dot(member, far_field, precision=HIGHEST).reshape(vesicles, 3, FAR)
    return gradient + jnp.pad(far_terms, ((0, 0), (0, 0), (0, coef_count - FAR)))


def solution(mesh):
    in_specs = (
        P("dev", None, None),
        P("dev", None, None),
        P("dev"),
        P("dev"),
        P("dev"),
        P("dev", None, None),
        P("dev", None, None),
        P("dev", None),
    )
    out_specs = P("dev", None, None)
    return jax.shard_map(
        on_device, mesh=mesh, in_specs=in_specs, out_specs=out_specs, check_vma=False
    )
```

```python
import functools
import math

import jax
import jax.numpy as jnp
import numpy as np
from jax import lax
from jax.experimental import pallas as pl
from jax.experimental.pallas import tpu as pltpu
from jax.sharding import PartitionSpec as P

NLAT = 24
NEAR_LAT = 8
REGIONS = 64
FAR = 8


HIGHEST = lax.Precision.HIGHEST


def harmonic_tables(grid_lat, degree_count):
    longitudes = 2 * grid_lat
    full_longitudes = 2 * degree_count
    colatitude = (np.arange(grid_lat, dtype=np.float64) + 0.5) * (math.pi / grid_lat)
    cosine = np.cos(colatitude)
    values = [np.ones_like(cosine), cosine]
    for degree in range(2, degree_count):
        values.append(((2 * degree - 1) * cosine * values[-1] - (degree - 1) * values[-2]) / degree)
    degrees = np.arange(degree_count, dtype=np.float64)
    legendre = np.stack(values[:degree_count], axis=1) * np.sqrt((2.0 * degrees + 1.0) / 2.0)
    azimuth = np.arange(longitudes, dtype=np.float64) * (2.0 * math.pi / longitudes)
    halfway = degree_count // 2
    mode_index = np.arange(degree_count, dtype=np.float64)
    frequency = np.where(mode_index < halfway, mode_index, mode_index - halfway + 1.0)
    phases = azimuth[:, None] * frequency[None, :]
    fourier = np.where(mode_index[None, :] < halfway, np.cos(phases), np.sin(phases))
    fourier = fourier * np.where(
        mode_index[None, :] == 0, math.sqrt(1.0 / full_longitudes), math.sqrt(2.0 / full_longitudes)
    )
    synthesis = np.einsum("jl,km->lmjk", legendre, fourier).reshape(
        degree_count * degree_count, grid_lat * longitudes
    )
    quadrature = np.repeat(np.sin(colatitude) * (math.pi / grid_lat), longitudes)
    degree_scale = np.repeat(1.0 / (2.0 * degrees + 1.0), degree_count)
    return (synthesis, quadrature, degree_scale)


def far_coupling(regions, vesicle_total):
    position = np.arange(regions, dtype=np.float64)
    return 1.0 / ((1.0 + np.abs(position[:, None] - position[None, :])) * math.sqrt(vesicle_total))


GROUP = 8

def gather_pair_kernel(
    t_stride, s_stride, live_ref, tidx_ref, sidx_ref, t_ref, s_ref, o_ref, order_ref, tile_ref
):
    pairs = live_ref.shape[0]
    scale = 1.0 / math.sqrt(t_ref.shape[1])
    o_ref[...] = jnp.zeros(o_ref.shape, o_ref.dtype)

    def pack(p, count):
        order_ref[count] = p
        return count + live_ref[p]

    count = lax.fori_loop(0, pairs, pack, 0, unroll=8)
    for j in range(GROUP):
        order_ref[count + j] = order_ref[0]

    def group_body(g, carry):
        picked = [order_ref[g * GROUP + j] for j in range(GROUP)]
        for j in range(GROUP):
            t_row = tidx_ref[picked[j]] * t_stride
            s_row = sidx_ref[picked[j]] * s_stride
            for k in range(6):
                tile_ref[k, pl.ds(j, 1), :] = t_ref[pl.ds(t_row + k, 1), :]
            for c in range(3):
                tile_ref[6 + c, pl.ds(j, 1), :] = s_ref[pl.ds(s_row + c, 1), :]
        t_cols = [tile_ref[c].T for c in range(3)]
        c_cols = [tile_ref[3 + c].T for c in range(3)]
        s_rows = [tile_ref[6 + c] for c in range(3)]
        for p in range(GROUP):
            distance = None
            for c in range(3):
                apart = t_cols[c][:, p : p + 1] - s_rows[c][p : p + 1, :]
                distance = apart * apart if distance is None else distance + apart * apart
            kernel_block = 1.0 / (1.0 + distance)
            for c in range(3):
                o_ref[c, pl.ds(picked[p], 1), :] = (
                    jnp.sum(c_cols[c][:, p : p + 1] * kernel_block, axis=0, keepdims=True) * scale
                )
        return carry

    lax.fori_loop(0, (count + GROUP - 1) // GROUP, group_body, 0)


def gather_pair_terms(live, target_index, source_index, target_rows, t_stride, source_rows, s_stride):
    pairs = live.shape[0]
    points = target_rows.shape[1]
    vmem = pl.BlockSpec(memory_space=pltpu.VMEM)
    smem = pl.BlockSpec(memory_space=pltpu.SMEM)
    return pl.pallas_call(
        functools.partial(gather_pair_kernel, t_stride, s_stride),
        in_specs=[smem, smem, smem, vmem, vmem],
        out_specs=vmem,
        out_shape=jax.ShapeDtypeStruct((3, pairs, points), jnp.float32),
        scratch_shapes=[pltpu.SMEM((pairs + GROUP,), jnp.int32), pltpu.VMEM((9, GROUP, points), jnp.float32)],
        name="gather_pair_terms",
    )(live, target_index, source_index, target_rows, source_rows)

def onehot(index, count):
    return (index[:, None] == jnp.arange(count, dtype=jnp.int32)[None, :]).astype(jnp.float32)


def on_device(
    cotangent, surface, region_id, local_target, local_shift, near_target, near_source, near_count
):
    vesicles = cotangent.shape[0]
    coef_count = cotangent.shape[2]
    devices = lax.axis_size("dev")
    slot_count = near_target.shape[2]
    pair_slots = devices * slot_count

    synthesis, quadrature, degree_scale = harmonic_tables(NLAT, NLAT)
    near_synthesis, near_quadrature, unused_scale = harmonic_tables(NEAR_LAT, NLAT)
    points = synthesis.shape[1]
    near_points = near_synthesis.shape[1]
    full = jnp.asarray(synthesis.astype(np.float32))
    near = jnp.asarray(near_synthesis.astype(np.float32))
    contract_rows = (((0,), (0,)), ((), ()))
    cot_flat = cotangent.reshape(vesicles * 3, coef_count)
    surface_flat = surface.reshape(vesicles * 3, coef_count)

    near_cot = jnp.dot(cot_flat, near, precision=HIGHEST).reshape(vesicles, 3, near_points)
    near_shape = jnp.dot(surface_flat, near, precision=HIGHEST).reshape(vesicles, 3, near_points)
    cot_points = jnp.dot(cot_flat, full, precision=HIGHEST).reshape(vesicles, 3, points)
    shape_points = jnp.dot(surface_flat, full, precision=HIGHEST).reshape(vesicles, 3, points)
    stretch = 1.0 / (1.0 + jnp.sum(shape_points * shape_points, axis=1))
    point_total = stretch[:, None, :] * cot_points * jnp.asarray(quadrature.astype(np.float32))
    contract_points = (((1,), (1,)), ((), ()))
    point_coefs = lax.dot_general(
        point_total.reshape(vesicles * 3, points), full, contract_points, precision=HIGHEST
    )
    gradient = lax.optimization_barrier(
        jnp.asarray(degree_scale.astype(np.float32)) * cotangent
        + point_coefs.reshape(cotangent.shape)
    )

    near_vkx = jnp.concatenate([near_shape, near_cot], axis=1)
    rows_per_vesicle = near_vkx.shape[1]
    near_flat = near_vkx.reshape(vesicles * rows_per_vesicle, near_points)

    targets = near_target[0].reshape(pair_slots)
    alive = (
        jnp.arange(slot_count, dtype=jnp.int32)[None, :] < near_count[0][:, None]
    ).reshape(pair_slots)
    picked = jnp.einsum("pv,vkx->pkx", onehot(targets, vesicles), near_vkx, precision=HIGHEST)
    kind = jnp.arange(rows_per_vesicle, dtype=jnp.int32)[None, :, None]
    picked = jnp.where((kind < 3) | alive[:, None, None], picked, 0.0)
    member = onehot(region_id, REGIONS)
    moments = cotangent[:, :, :FAR].reshape(vesicles, 3 * FAR)
    partial_far = lax.dot_general(member, moments, contract_rows, precision=HIGHEST)
    far_rows = REGIONS * 3 * FAR // (slot_count * near_points)
    far_block = partial_far.reshape(1, slot_count, far_rows, near_points)
    far_block = jnp.broadcast_to(far_block, (devices, slot_count, far_rows, near_points))
    pair_rows = rows_per_vesicle + far_rows
    outgoing = jnp.concatenate(
        [picked, far_block.reshape(pair_slots, far_rows, near_points)], axis=1
    ).reshape(pair_slots * pair_rows, near_points)
    incoming = lax.all_to_all(outgoing, "dev", split_axis=0, concat_axis=0, tiled=True)
    peer_rows = jnp.sum(incoming.reshape(devices, slot_count * pair_rows, near_points), axis=0)
    far_total = peer_rows.reshape(slot_count, pair_rows, near_points)[:, rows_per_vesicle:, :]
    far_total = far_total.reshape(REGIONS, 3 * FAR)
    sources = jnp.clip(near_source[0].reshape(pair_slots), 0, vesicles - 1)
    source_onehot = onehot(sources, vesicles)

    local_target = jnp.clip(local_target, 0, vesicles - 1)
    local_source = (local_target + local_shift) % vesicles
    local_onehot = onehot(local_source, vesicles)
    local_terms = gather_pair_terms(
        jnp.ones((vesicles,), jnp.int32),
        local_target,
        local_source,
        near_flat,
        rows_per_vesicle,
        near_flat,
        rows_per_vesicle,
    )
    row_size = jnp.max(jnp.abs(incoming), axis=1).reshape(pair_slots, pair_rows)
    live = (jnp.max(row_size[:, 3:rows_per_vesicle], axis=1) > 0.0).astype(jnp.int32)
    remote_terms = gather_pair_terms(
        live,
        jnp.arange(pair_slots, dtype=jnp.int32),
        sources,
        incoming,
        pair_rows,
        near_flat,
        rows_per_vesicle,
    )
    near_total = jnp.einsum(
        "pv,kpx->vkx", local_onehot, local_terms, precision=HIGHEST
    ) + jnp.einsum("pv,kpx->vkx", source_onehot, remote_terms, precision=HIGHEST)

    near_weighted = near_total.reshape(vesicles * 3, near_points) * jnp.asarray(
        near_quadrature.astype(np.float32)
    )
    gradient = gradient + lax.dot_general(
        near_weighted, near, contract_points, precision=HIGHEST
    ).reshape(cotangent.shape)

    coupling = jnp.asarray(far_coupling(REGIONS, vesicles * devices).astype(np.float32))
    far_field = lax.dot_general(coupling, far_total, contract_rows, precision=HIGHEST)
    far_terms = jnp.dot(member, far_field, precision=HIGHEST).reshape(vesicles, 3, FAR)
    return gradient + jnp.pad(far_terms, ((0, 0), (0, 0), (0, coef_count - FAR)))


def solution(mesh):
    in_specs = (
        P("dev", None, None),
        P("dev", None, None),
        P("dev"),
        P("dev"),
        P("dev"),
        P("dev", None, None),
        P("dev", None, None),
        P("dev", None),
    )
    out_specs = P("dev", None, None)
    return jax.shard_map(
        on_device, mesh=mesh, in_specs=in_specs, out_specs=out_specs, check_vma=False
    )
```

```python
import functools
import math

import jax
import jax.numpy as jnp
import numpy as np
from jax import lax
from jax.experimental import pallas as pl
from jax.experimental.pallas import tpu as pltpu
from jax.sharding import PartitionSpec as P

NLAT = 24
NEAR_LAT = 8
REGIONS = 64
FAR = 8


HIGHEST = lax.Precision.HIGHEST


def harmonic_tables(grid_lat, degree_count):
    longitudes = 2 * grid_lat
    full_longitudes = 2 * degree_count
    colatitude = (np.arange(grid_lat, dtype=np.float64) + 0.5) * (math.pi / grid_lat)
    cosine = np.cos(colatitude)
    values = [np.ones_like(cosine), cosine]
    for degree in range(2, degree_count):
        values.append(((2 * degree - 1) * cosine * values[-1] - (degree - 1) * values[-2]) / degree)
    degrees = np.arange(degree_count, dtype=np.float64)
    legendre = np.stack(values[:degree_count], axis=1) * np.sqrt((2.0 * degrees + 1.0) / 2.0)
    azimuth = np.arange(longitudes, dtype=np.float64) * (2.0 * math.pi / longitudes)
    halfway = degree_count // 2
    mode_index = np.arange(degree_count, dtype=np.float64)
    frequency = np.where(mode_index < halfway, mode_index, mode_index - halfway + 1.0)
    phases = azimuth[:, None] * frequency[None, :]
    fourier = np.where(mode_index[None, :] < halfway, np.cos(phases), np.sin(phases))
    fourier = fourier * np.where(
        mode_index[None, :] == 0, math.sqrt(1.0 / full_longitudes), math.sqrt(2.0 / full_longitudes)
    )
    synthesis = np.einsum("jl,km->lmjk", legendre, fourier).reshape(
        degree_count * degree_count, grid_lat * longitudes
    )
    quadrature = np.repeat(np.sin(colatitude) * (math.pi / grid_lat), longitudes)
    degree_scale = np.repeat(1.0 / (2.0 * degrees + 1.0), degree_count)
    return (synthesis, quadrature, degree_scale)


def far_coupling(regions, vesicle_total):
    position = np.arange(regions, dtype=np.float64)
    return 1.0 / ((1.0 + np.abs(position[:, None] - position[None, :])) * math.sqrt(vesicle_total))


GROUP = 8
STEP = 16

def gather_pair_kernel(
    t_stride, s_stride, live_ref, tidx_ref, sidx_ref, t_ref, s_ref, o_ref, order_ref, tile_ref
):
    pairs = live_ref.shape[0]
    scale = 1.0 / math.sqrt(t_ref.shape[1])
    o_ref[...] = jnp.zeros(o_ref.shape, o_ref.dtype)

    def pack(p, count):
        order_ref[count] = p
        return count + live_ref[p]

    count = lax.fori_loop(0, pairs, pack, 0, unroll=8)
    for j in range(STEP):
        order_ref[count + j] = order_ref[0]

    def group_body(g, carry):
        picked = [order_ref[g * STEP + j] for j in range(STEP)]
        for j in range(STEP):
            t_row = tidx_ref[picked[j]] * t_stride
            s_row = sidx_ref[picked[j]] * s_stride
            half, row = divmod(j, GROUP)
            for k in range(6):
                tile_ref[half, k, pl.ds(row, 1), :] = t_ref[pl.ds(t_row + k, 1), :]
            for c in range(3):
                tile_ref[half, 6 + c, pl.ds(row, 1), :] = s_ref[pl.ds(s_row + c, 1), :]
        for half in range(STEP // GROUP):
            t_cols = [tile_ref[half, c].T for c in range(3)]
            c_cols = [tile_ref[half, 3 + c].T for c in range(3)]
            s_rows = [tile_ref[half, 6 + c] for c in range(3)]
            for p in range(GROUP):
                distance = None
                for c in range(3):
                    apart = t_cols[c][:, p : p + 1] - s_rows[c][p : p + 1, :]
                    distance = apart * apart if distance is None else distance + apart * apart
                kernel_block = 1.0 / (1.0 + distance)
                for c in range(3):
                    o_ref[c, pl.ds(picked[half * GROUP + p], 1), :] = (
                        jnp.sum(c_cols[c][:, p : p + 1] * kernel_block, axis=0, keepdims=True)
                        * scale
                    )
        return carry

    lax.fori_loop(0, (count + STEP - 1) // STEP, group_body, 0)


def gather_pair_terms(live, target_index, source_index, target_rows, t_stride, source_rows, s_stride):
    pairs = live.shape[0]
    points = target_rows.shape[1]
    vmem = pl.BlockSpec(memory_space=pltpu.VMEM)
    smem = pl.BlockSpec(memory_space=pltpu.SMEM)
    return pl.pallas_call(
        functools.partial(gather_pair_kernel, t_stride, s_stride),
        in_specs=[smem, smem, smem, vmem, vmem],
        out_specs=vmem,
        out_shape=jax.ShapeDtypeStruct((3, pairs, points), jnp.float32),
        scratch_shapes=[pltpu.SMEM((pairs + STEP,), jnp.int32), pltpu.VMEM((STEP // GROUP, 9, GROUP, points), jnp.float32)],
        name="gather_pair_terms",
    )(live, target_index, source_index, target_rows, source_rows)

def onehot(index, count):
    return (index[:, None] == jnp.arange(count, dtype=jnp.int32)[None, :]).astype(jnp.float32)


def on_device(
    cotangent, surface, region_id, local_target, local_shift, near_target, near_source, near_count
):
    vesicles = cotangent.shape[0]
    coef_count = cotangent.shape[2]
    devices = lax.axis_size("dev")
    slot_count = near_target.shape[2]
    pair_slots = devices * slot_count

    synthesis, quadrature, degree_scale = harmonic_tables(NLAT, NLAT)
    near_synthesis, near_quadrature, unused_scale = harmonic_tables(NEAR_LAT, NLAT)
    points = synthesis.shape[1]
    near_points = near_synthesis.shape[1]
    full = jnp.asarray(synthesis.astype(np.float32))
    near = jnp.asarray(near_synthesis.astype(np.float32))
    contract_rows = (((0,), (0,)), ((), ()))
    cot_flat = cotangent.reshape(vesicles * 3, coef_count)
    surface_flat = surface.reshape(vesicles * 3, coef_count)

    near_cot = jnp.dot(cot_flat, near, precision=HIGHEST).reshape(vesicles, 3, near_points)
    near_shape = jnp.dot(surface_flat, near, precision=HIGHEST).reshape(vesicles, 3, near_points)
    cot_points = jnp.dot(cot_flat, full, precision=HIGHEST).reshape(vesicles, 3, points)
    shape_points = jnp.dot(surface_flat, full, precision=HIGHEST).reshape(vesicles, 3, points)
    stretch = 1.0 / (1.0 + jnp.sum(shape_points * shape_points, axis=1))
    point_total = stretch[:, None, :] * cot_points * jnp.asarray(quadrature.astype(np.float32))
    contract_points = (((1,), (1,)), ((), ()))
    point_coefs = lax.dot_general(
        point_total.reshape(vesicles * 3, points), full, contract_points, precision=HIGHEST
    )
    gradient = lax.optimization_barrier(
        jnp.asarray(degree_scale.astype(np.float32)) * cotangent
        + point_coefs.reshape(cotangent.shape)
    )

    near_vkx = jnp.concatenate([near_shape, near_cot], axis=1)
    rows_per_vesicle = near_vkx.shape[1]
    near_flat = near_vkx.reshape(vesicles * rows_per_vesicle, near_points)

    targets = near_target[0].reshape(pair_slots)
    alive = (
        jnp.arange(slot_count, dtype=jnp.int32)[None, :] < near_count[0][:, None]
    ).reshape(pair_slots)
    picked = jnp.einsum("pv,vkx->pkx", onehot(targets, vesicles), near_vkx, precision=HIGHEST)
    kind = jnp.arange(rows_per_vesicle, dtype=jnp.int32)[None, :, None]
    picked = jnp.where((kind < 3) | alive[:, None, None], picked, 0.0)
    member = onehot(region_id, REGIONS)
    moments = cotangent[:, :, :FAR].reshape(vesicles, 3 * FAR)
    partial_far = lax.dot_general(member, moments, contract_rows, precision=HIGHEST)
    far_rows = REGIONS * 3 * FAR // (slot_count * near_points)
    far_block = partial_far.reshape(1, slot_count, far_rows, near_points)
    far_block = jnp.broadcast_to(far_block, (devices, slot_count, far_rows, near_points))
    pair_rows = rows_per_vesicle + far_rows
    outgoing = jnp.concatenate(
        [picked, far_block.reshape(pair_slots, far_rows, near_points)], axis=1
    ).reshape(pair_slots * pair_rows, near_points)
    incoming = lax.all_to_all(outgoing, "dev", split_axis=0, concat_axis=0, tiled=True)
    peer_rows = jnp.sum(incoming.reshape(devices, slot_count * pair_rows, near_points), axis=0)
    far_total = peer_rows.reshape(slot_count, pair_rows, near_points)[:, rows_per_vesicle:, :]
    far_total = far_total.reshape(REGIONS, 3 * FAR)
    sources = jnp.clip(near_source[0].reshape(pair_slots), 0, vesicles - 1)
    source_onehot = onehot(sources, vesicles)

    local_target = jnp.clip(local_target, 0, vesicles - 1)
    local_source = (local_target + local_shift) % vesicles
    local_onehot = onehot(local_source, vesicles)
    local_terms = gather_pair_terms(
        jnp.ones((vesicles,), jnp.int32),
        local_target,
        local_source,
        near_flat,
        rows_per_vesicle,
        near_flat,
        rows_per_vesicle,
    )
    row_size = jnp.max(jnp.abs(incoming), axis=1).reshape(pair_slots, pair_rows)
    live = (jnp.max(row_size[:, 3:rows_per_vesicle], axis=1) > 0.0).astype(jnp.int32)
    remote_terms = gather_pair_terms(
        live,
        jnp.arange(pair_slots, dtype=jnp.int32),
        sources,
        incoming,
        pair_rows,
        near_flat,
        rows_per_vesicle,
    )
    near_total = jnp.einsum(
        "pv,kpx->vkx", local_onehot, local_terms, precision=HIGHEST
    ) + jnp.einsum("pv,kpx->vkx", source_onehot, remote_terms, precision=HIGHEST)

    near_weighted = near_total.reshape(vesicles * 3, near_points) * jnp.asarray(
        near_quadrature.astype(np.float32)
    )
    gradient = gradient + lax.dot_general(
        near_weighted, near, contract_points, precision=HIGHEST
    ).reshape(cotangent.shape)

    coupling = jnp.asarray(far_coupling(REGIONS, vesicles * devices).astype(np.float32))
    far_field = lax.dot_general(coupling, far_total, contract_rows, precision=HIGHEST)
    far_terms = jnp.dot(member, far_field, precision=HIGHEST).reshape(vesicles, 3, FAR)
    return gradient + jnp.pad(far_terms, ((0, 0), (0, 0), (0, coef_count - FAR)))


def solution(mesh):
    in_specs = (
        P("dev", None, None),
        P("dev", None, None),
        P("dev"),
        P("dev"),
        P("dev"),
        P("dev", None, None),
        P("dev", None, None),
        P("dev", None),
    )
    out_specs = P("dev", None, None)
    return jax.shard_map(
        on_device, mesh=mesh, in_specs=in_specs, out_specs=out_specs, check_vma=False
    )
```

```python
import functools
import math

import jax
import jax.numpy as jnp
import numpy as np
from jax import lax
from jax.experimental import pallas as pl
from jax.experimental.pallas import tpu as pltpu
from jax.sharding import PartitionSpec as P

NLAT = 24
NEAR_LAT = 8
REGIONS = 64
FAR = 8


HIGHEST = lax.Precision.HIGHEST


def harmonic_tables(grid_lat, degree_count):
    longitudes = 2 * grid_lat
    full_longitudes = 2 * degree_count
    colatitude = (np.arange(grid_lat, dtype=np.float64) + 0.5) * (math.pi / grid_lat)
    cosine = np.cos(colatitude)
    values = [np.ones_like(cosine), cosine]
    for degree in range(2, degree_count):
        values.append(((2 * degree - 1) * cosine * values[-1] - (degree - 1) * values[-2]) / degree)
    degrees = np.arange(degree_count, dtype=np.float64)
    legendre = np.stack(values[:degree_count], axis=1) * np.sqrt((2.0 * degrees + 1.0) / 2.0)
    azimuth = np.arange(longitudes, dtype=np.float64) * (2.0 * math.pi / longitudes)
    halfway = degree_count // 2
    mode_index = np.arange(degree_count, dtype=np.float64)
    frequency = np.where(mode_index < halfway, mode_index, mode_index - halfway + 1.0)
    phases = azimuth[:, None] * frequency[None, :]
    fourier = np.where(mode_index[None, :] < halfway, np.cos(phases), np.sin(phases))
    fourier = fourier * np.where(
        mode_index[None, :] == 0, math.sqrt(1.0 / full_longitudes), math.sqrt(2.0 / full_longitudes)
    )
    synthesis = np.einsum("jl,km->lmjk", legendre, fourier).reshape(
        degree_count * degree_count, grid_lat * longitudes
    )
    quadrature = np.repeat(np.sin(colatitude) * (math.pi / grid_lat), longitudes)
    degree_scale = np.repeat(1.0 / (2.0 * degrees + 1.0), degree_count)
    return (synthesis, quadrature, degree_scale)


def far_coupling(regions, vesicle_total):
    position = np.arange(regions, dtype=np.float64)
    return 1.0 / ((1.0 + np.abs(position[:, None] - position[None, :])) * math.sqrt(vesicle_total))


GROUP = 8

def gather_pair_kernel(
    t_stride, s_stride, live_ref, tidx_ref, sidx_ref, t_ref, s_ref, o_ref, order_ref, tile_ref
):
    pairs = live_ref.shape[0]
    scale = 1.0 / math.sqrt(t_ref.shape[1])
    o_ref[...] = jnp.zeros(o_ref.shape, o_ref.dtype)

    def pack(p, count):
        order_ref[count] = p
        return count + live_ref[p]

    count = lax.fori_loop(0, pairs, pack, 0, unroll=8)
    for j in range(GROUP):
        order_ref[count + j] = order_ref[0]

    def group_body(g, carry):
        picked = [order_ref[g * GROUP + j] for j in range(GROUP)]
        for j in range(GROUP):
            t_row = tidx_ref[picked[j]] * t_stride
            s_row = sidx_ref[picked[j]] * s_stride
            for k in range(6):
                tile_ref[k, pl.ds(j, 1), :] = t_ref[pl.ds(t_row + k, 1), :]
            for c in range(3):
                tile_ref[6 + c, pl.ds(j, 1), :] = s_ref[pl.ds(s_row + c, 1), :]
        t_cols = [tile_ref[c].T for c in range(3)]
        c_cols = [tile_ref[3 + c].T for c in range(3)]
        s_rows = [tile_ref[6 + c] for c in range(3)]
        for p in range(GROUP):
            distance = None
            for c in range(3):
                apart = t_cols[c][:, p : p + 1] - s_rows[c][p : p + 1, :]
                distance = apart * apart if distance is None else distance + apart * apart
            base = 1.0 + distance
            kernel_block = pl.reciprocal(base, approx=True)
            kernel_block = kernel_block * (2.0 - base * kernel_block)
            kernel_block = kernel_block * (2.0 - base * kernel_block)
            for c in range(3):
                o_ref[c, pl.ds(picked[p], 1), :] = (
                    jnp.sum(c_cols[c][:, p : p + 1] * kernel_block, axis=0, keepdims=True) * scale
                )
        return carry

    lax.fori_loop(0, (count + GROUP - 1) // GROUP, group_body, 0)


def gather_pair_terms(live, target_index, source_index, target_rows, t_stride, source_rows, s_stride):
    pairs = live.shape[0]
    points = target_rows.shape[1]
    vmem = pl.BlockSpec(memory_space=pltpu.VMEM)
    smem = pl.BlockSpec(memory_space=pltpu.SMEM)
    return pl.pallas_call(
        functools.partial(gather_pair_kernel, t_stride, s_stride),
        in_specs=[smem, smem, smem, vmem, vmem],
        out_specs=vmem,
        out_shape=jax.ShapeDtypeStruct((3, pairs, points), jnp.float32),
        scratch_shapes=[pltpu.SMEM((pairs + GROUP,), jnp.int32), pltpu.VMEM((9, GROUP, points), jnp.float32)],
        name="gather_pair_terms",
    )(live, target_index, source_index, target_rows, source_rows)

def onehot(index, count):
    return (index[:, None] == jnp.arange(count, dtype=jnp.int32)[None, :]).astype(jnp.float32)


def on_device(
    cotangent, surface, region_id, local_target, local_shift, near_target, near_source, near_count
):
    vesicles = cotangent.shape[0]
    coef_count = cotangent.shape[2]
    devices = lax.axis_size("dev")
    slot_count = near_target.shape[2]
    pair_slots = devices * slot_count

    synthesis, quadrature, degree_scale = harmonic_tables(NLAT, NLAT)
    near_synthesis, near_quadrature, unused_scale = harmonic_tables(NEAR_LAT, NLAT)
    points = synthesis.shape[1]
    near_points = near_synthesis.shape[1]
    full = jnp.asarray(synthesis.astype(np.float32))
    near = jnp.asarray(near_synthesis.astype(np.float32))
    contract_rows = (((0,), (0,)), ((), ()))
    cot_flat = cotangent.reshape(vesicles * 3, coef_count)
    surface_flat = surface.reshape(vesicles * 3, coef_count)

    near_cot = jnp.dot(cot_flat, near, precision=HIGHEST).reshape(vesicles, 3, near_points)
    near_shape = jnp.dot(surface_flat, near, precision=HIGHEST).reshape(vesicles, 3, near_points)
    cot_points = jnp.dot(cot_flat, full, precision=HIGHEST).reshape(vesicles, 3, points)
    shape_points = jnp.dot(surface_flat, full, precision=HIGHEST).reshape(vesicles, 3, points)
    stretch = 1.0 / (1.0 + jnp.sum(shape_points * shape_points, axis=1))
    point_total = stretch[:, None, :] * cot_points * jnp.asarray(quadrature.astype(np.float32))
    contract_points = (((1,), (1,)), ((), ()))
    point_coefs = lax.dot_general(
        point_total.reshape(vesicles * 3, points), full, contract_points, precision=HIGHEST
    )
    gradient = lax.optimization_barrier(
        jnp.asarray(degree_scale.astype(np.float32)) * cotangent
        + point_coefs.reshape(cotangent.shape)
    )

    near_vkx = jnp.concatenate([near_shape, near_cot], axis=1)
    rows_per_vesicle = near_vkx.shape[1]
    near_flat = near_vkx.reshape(vesicles * rows_per_vesicle, near_points)

    targets = near_target[0].reshape(pair_slots)
    alive = (
        jnp.arange(slot_count, dtype=jnp.int32)[None, :] < near_count[0][:, None]
    ).reshape(pair_slots)
    picked = jnp.einsum("pv,vkx->pkx", onehot(targets, vesicles), near_vkx, precision=HIGHEST)
    kind = jnp.arange(rows_per_vesicle, dtype=jnp.int32)[None, :, None]
    picked = jnp.where((kind < 3) | alive[:, None, None], picked, 0.0)
    member = onehot(region_id, REGIONS)
    moments = cotangent[:, :, :FAR].reshape(vesicles, 3 * FAR)
    partial_far = lax.dot_general(member, moments, contract_rows, precision=HIGHEST)
    far_rows = REGIONS * 3 * FAR // (slot_count * near_points)
    far_block = partial_far.reshape(1, slot_count, far_rows, near_points)
    far_block = jnp.broadcast_to(far_block, (devices, slot_count, far_rows, near_points))
    pair_rows = rows_per_vesicle + far_rows
    outgoing = jnp.concatenate(
        [picked, far_block.reshape(pair_slots, far_rows, near_points)], axis=1
    ).reshape(pair_slots * pair_rows, near_points)
    incoming = lax.all_to_all(outgoing, "dev", split_axis=0, concat_axis=0, tiled=True)
    peer_rows = jnp.sum(incoming.reshape(devices, slot_count * pair_rows, near_points), axis=0)
    far_total = peer_rows.reshape(slot_count, pair_rows, near_points)[:, rows_per_vesicle:, :]
    far_total = far_total.reshape(REGIONS, 3 * FAR)
    sources = jnp.clip(near_source[0].reshape(pair_slots), 0, vesicles - 1)
    source_onehot = onehot(sources, vesicles)

    local_target = jnp.clip(local_target, 0, vesicles - 1)
    local_source = (local_target + local_shift) % vesicles
    local_onehot = onehot(local_source, vesicles)
    local_terms = gather_pair_terms(
        jnp.ones((vesicles,), jnp.int32),
        local_target,
        local_source,
        near_flat,
        rows_per_vesicle,
        near_flat,
        rows_per_vesicle,
    )
    row_size = jnp.max(jnp.abs(incoming), axis=1).reshape(pair_slots, pair_rows)
    live = (jnp.max(row_size[:, 3:rows_per_vesicle], axis=1) > 0.0).astype(jnp.int32)
    remote_terms = gather_pair_terms(
        live,
        jnp.arange(pair_slots, dtype=jnp.int32),
        sources,
        incoming,
        pair_rows,
        near_flat,
        rows_per_vesicle,
    )
    near_total = jnp.einsum(
        "pv,kpx->vkx", local_onehot, local_terms, precision=HIGHEST
    ) + jnp.einsum("pv,kpx->vkx", source_onehot, remote_terms, precision=HIGHEST)

    near_weighted = near_total.reshape(vesicles * 3, near_points) * jnp.asarray(
        near_quadrature.astype(np.float32)
    )
    gradient = gradient + lax.dot_general(
        near_weighted, near, contract_points, precision=HIGHEST
    ).reshape(cotangent.shape)

    coupling = jnp.asarray(far_coupling(REGIONS, vesicles * devices).astype(np.float32))
    far_field = lax.dot_general(coupling, far_total, contract_rows, precision=HIGHEST)
    far_terms = jnp.dot(member, far_field, precision=HIGHEST).reshape(vesicles, 3, FAR)
    return gradient + jnp.pad(far_terms, ((0, 0), (0, 0), (0, coef_count - FAR)))


def solution(mesh):
    in_specs = (
        P("dev", None, None),
        P("dev", None, None),
        P("dev"),
        P("dev"),
        P("dev"),
        P("dev", None, None),
        P("dev", None, None),
        P("dev", None),
    )
    out_specs = P("dev", None, None)
    return jax.shard_map(
        on_device, mesh=mesh, in_specs=in_specs, out_specs=out_specs, check_vma=False
    )
```

```python
import functools
import math

import jax
import jax.numpy as jnp
import numpy as np
from jax import lax
from jax.experimental import pallas as pl
from jax.experimental.pallas import tpu as pltpu
from jax.sharding import PartitionSpec as P

NLAT = 24
NEAR_LAT = 8
REGIONS = 64
FAR = 8


HIGHEST = lax.Precision.HIGHEST


def harmonic_tables(grid_lat, degree_count):
    longitudes = 2 * grid_lat
    full_longitudes = 2 * degree_count
    colatitude = (np.arange(grid_lat, dtype=np.float64) + 0.5) * (math.pi / grid_lat)
    cosine = np.cos(colatitude)
    values = [np.ones_like(cosine), cosine]
    for degree in range(2, degree_count):
        values.append(((2 * degree - 1) * cosine * values[-1] - (degree - 1) * values[-2]) / degree)
    degrees = np.arange(degree_count, dtype=np.float64)
    legendre = np.stack(values[:degree_count], axis=1) * np.sqrt((2.0 * degrees + 1.0) / 2.0)
    azimuth = np.arange(longitudes, dtype=np.float64) * (2.0 * math.pi / longitudes)
    halfway = degree_count // 2
    mode_index = np.arange(degree_count, dtype=np.float64)
    frequency = np.where(mode_index < halfway, mode_index, mode_index - halfway + 1.0)
    phases = azimuth[:, None] * frequency[None, :]
    fourier = np.where(mode_index[None, :] < halfway, np.cos(phases), np.sin(phases))
    fourier = fourier * np.where(
        mode_index[None, :] == 0, math.sqrt(1.0 / full_longitudes), math.sqrt(2.0 / full_longitudes)
    )
    synthesis = np.einsum("jl,km->lmjk", legendre, fourier).reshape(
        degree_count * degree_count, grid_lat * longitudes
    )
    quadrature = np.repeat(np.sin(colatitude) * (math.pi / grid_lat), longitudes)
    degree_scale = np.repeat(1.0 / (2.0 * degrees + 1.0), degree_count)
    return (synthesis, quadrature, degree_scale)


def far_coupling(regions, vesicle_total):
    position = np.arange(regions, dtype=np.float64)
    return 1.0 / ((1.0 + np.abs(position[:, None] - position[None, :])) * math.sqrt(vesicle_total))


GROUP = 8

def gather_pair_kernel(
    t_stride, s_stride, live_ref, tidx_ref, sidx_ref, t_ref, s_ref, o_ref, order_ref, tile_ref, cot_ref
):
    pairs = live_ref.shape[0]
    scale = 1.0 / math.sqrt(t_ref.shape[1])
    o_ref[...] = jnp.zeros(o_ref.shape, o_ref.dtype)
    cot_ref[...] = jnp.zeros(cot_ref.shape, cot_ref.dtype)

    def pack(p, count):
        order_ref[count] = p
        return count + live_ref[p]

    count = lax.fori_loop(0, pairs, pack, 0, unroll=8)
    for j in range(GROUP):
        order_ref[count + j] = order_ref[0]

    def group_body(g, carry):
        picked = [order_ref[g * GROUP + j] for j in range(GROUP)]
        for j in range(GROUP):
            t_row = tidx_ref[picked[j]] * t_stride
            s_row = sidx_ref[picked[j]] * s_stride
            for c in range(3):
                tile_ref[c, pl.ds(j, 1), :] = t_ref[pl.ds(t_row + c, 1), :]
                cot_ref[j, pl.ds(c, 1), :] = t_ref[pl.ds(t_row + 3 + c, 1), :]
                tile_ref[3 + c, pl.ds(j, 1), :] = s_ref[pl.ds(s_row + c, 1), :]
        t_cols = [tile_ref[c].T for c in range(3)]
        s_rows = [tile_ref[3 + c] for c in range(3)]
        for p in range(GROUP):
            distance = None
            for c in range(3):
                apart = t_cols[c][:, p : p + 1] - s_rows[c][p : p + 1, :]
                distance = apart * apart if distance is None else distance + apart * apart
            kernel_block = 1.0 / (1.0 + distance)
            terms = jnp.dot(
                cot_ref[p], kernel_block, precision=HIGHEST, preferred_element_type=jnp.float32
            )
            for c in range(3):
                o_ref[c, pl.ds(picked[p], 1), :] = terms[c : c + 1, :] * scale
        return carry

    lax.fori_loop(0, (count + GROUP - 1) // GROUP, group_body, 0)


def gather_pair_terms(live, target_index, source_index, target_rows, t_stride, source_rows, s_stride):
    pairs = live.shape[0]
    points = target_rows.shape[1]
    vmem = pl.BlockSpec(memory_space=pltpu.VMEM)
    smem = pl.BlockSpec(memory_space=pltpu.SMEM)
    return pl.pallas_call(
        functools.partial(gather_pair_kernel, t_stride, s_stride),
        in_specs=[smem, smem, smem, vmem, vmem],
        out_specs=vmem,
        out_shape=jax.ShapeDtypeStruct((3, pairs, points), jnp.float32),
        scratch_shapes=[pltpu.SMEM((pairs + GROUP,), jnp.int32),
            pltpu.VMEM((6, GROUP, points), jnp.float32),
            pltpu.VMEM((GROUP, 8, points), jnp.float32),
        ],
        name="gather_pair_terms",
    )(live, target_index, source_index, target_rows, source_rows)

def onehot(index, count):
    return (index[:, None] == jnp.arange(count, dtype=jnp.int32)[None, :]).astype(jnp.float32)


def on_device(
    cotangent, surface, region_id, local_target, local_shift, near_target, near_source, near_count
):
    vesicles = cotangent.shape[0]
    coef_count = cotangent.shape[2]
    devices = lax.axis_size("dev")
    slot_count = near_target.shape[2]
    pair_slots = devices * slot_count

    synthesis, quadrature, degree_scale = harmonic_tables(NLAT, NLAT)
    near_synthesis, near_quadrature, unused_scale = harmonic_tables(NEAR_LAT, NLAT)
    points = synthesis.shape[1]
    near_points = near_synthesis.shape[1]
    full = jnp.asarray(synthesis.astype(np.float32))
    near = jnp.asarray(near_synthesis.astype(np.float32))
    contract_rows = (((0,), (0,)), ((), ()))
    cot_flat = cotangent.reshape(vesicles * 3, coef_count)
    surface_flat = surface.reshape(vesicles * 3, coef_count)

    near_cot = jnp.dot(cot_flat, near, precision=HIGHEST).reshape(vesicles, 3, near_points)
    near_shape = jnp.dot(surface_flat, near, precision=HIGHEST).reshape(vesicles, 3, near_points)
    cot_points = jnp.dot(cot_flat, full, precision=HIGHEST).reshape(vesicles, 3, points)
    shape_points = jnp.dot(surface_flat, full, precision=HIGHEST).reshape(vesicles, 3, points)
    stretch = 1.0 / (1.0 + jnp.sum(shape_points * shape_points, axis=1))
    point_total = stretch[:, None, :] * cot_points * jnp.asarray(quadrature.astype(np.float32))
    contract_points = (((1,), (1,)), ((), ()))
    point_coefs = lax.dot_general(
        point_total.reshape(vesicles * 3, points), full, contract_points, precision=HIGHEST
    )
    gradient = lax.optimization_barrier(
        jnp.asarray(degree_scale.astype(np.float32)) * cotangent
        + point_coefs.reshape(cotangent.shape)
    )

    near_vkx = jnp.concatenate([near_shape, near_cot], axis=1)
    rows_per_vesicle = near_vkx.shape[1]
    near_flat = near_vkx.reshape(vesicles * rows_per_vesicle, near_points)

    targets = near_target[0].reshape(pair_slots)
    alive = (
        jnp.arange(slot_count, dtype=jnp.int32)[None, :] < near_count[0][:, None]
    ).reshape(pair_slots)
    picked = jnp.einsum("pv,vkx->pkx", onehot(targets, vesicles), near_vkx, precision=HIGHEST)
    kind = jnp.arange(rows_per_vesicle, dtype=jnp.int32)[None, :, None]
    picked = jnp.where((kind < 3) | alive[:, None, None], picked, 0.0)
    member = onehot(region_id, REGIONS)
    moments = cotangent[:, :, :FAR].reshape(vesicles, 3 * FAR)
    partial_far = lax.dot_general(member, moments, contract_rows, precision=HIGHEST)
    far_rows = REGIONS * 3 * FAR // (slot_count * near_points)
    far_block = partial_far.reshape(1, slot_count, far_rows, near_points)
    far_block = jnp.broadcast_to(far_block, (devices, slot_count, far_rows, near_points))
    pair_rows = rows_per_vesicle + far_rows
    outgoing = jnp.concatenate(
        [picked, far_block.reshape(pair_slots, far_rows, near_points)], axis=1
    ).reshape(pair_slots * pair_rows, near_points)
    incoming = lax.all_to_all(outgoing, "dev", split_axis=0, concat_axis=0, tiled=True)
    peer_rows = jnp.sum(incoming.reshape(devices, slot_count * pair_rows, near_points), axis=0)
    far_total = peer_rows.reshape(slot_count, pair_rows, near_points)[:, rows_per_vesicle:, :]
    far_total = far_total.reshape(REGIONS, 3 * FAR)
    sources = jnp.clip(near_source[0].reshape(pair_slots), 0, vesicles - 1)
    source_onehot = onehot(sources, vesicles)

    local_target = jnp.clip(local_target, 0, vesicles - 1)
    local_source = (local_target + local_shift) % vesicles
    local_onehot = onehot(local_source, vesicles)
    local_terms = gather_pair_terms(
        jnp.ones((vesicles,), jnp.int32),
        local_target,
        local_source,
        near_flat,
        rows_per_vesicle,
        near_flat,
        rows_per_vesicle,
    )
    row_size = jnp.max(jnp.abs(incoming), axis=1).reshape(pair_slots, pair_rows)
    live = (jnp.max(row_size[:, 3:rows_per_vesicle], axis=1) > 0.0).astype(jnp.int32)
    remote_terms = gather_pair_terms(
        live,
        jnp.arange(pair_slots, dtype=jnp.int32),
        sources,
        incoming,
        pair_rows,
        near_flat,
        rows_per_vesicle,
    )
    near_total = jnp.einsum(
        "pv,kpx->vkx", local_onehot, local_terms, precision=HIGHEST
    ) + jnp.einsum("pv,kpx->vkx", source_onehot, remote_terms, precision=HIGHEST)

    near_weighted = near_total.reshape(vesicles * 3, near_points) * jnp.asarray(
        near_quadrature.astype(np.float32)
    )
    gradient = gradient + lax.dot_general(
        near_weighted, near, contract_points, precision=HIGHEST
    ).reshape(cotangent.shape)

    coupling = jnp.asarray(far_coupling(REGIONS, vesicles * devices).astype(np.float32))
    far_field = lax.dot_general(coupling, far_total, contract_rows, precision=HIGHEST)
    far_terms = jnp.dot(member, far_field, precision=HIGHEST).reshape(vesicles, 3, FAR)
    return gradient + jnp.pad(far_terms, ((0, 0), (0, 0), (0, coef_count - FAR)))


def solution(mesh):
    in_specs = (
        P("dev", None, None),
        P("dev", None, None),
        P("dev"),
        P("dev"),
        P("dev"),
        P("dev", None, None),
        P("dev", None, None),
        P("dev", None),
    )
    out_specs = P("dev", None, None)
    return jax.shard_map(
        on_device, mesh=mesh, in_specs=in_specs, out_specs=out_specs, check_vma=False
    )
```

```python
import functools
import math

import jax
import jax.numpy as jnp
import numpy as np
from jax import lax
from jax.experimental import pallas as pl
from jax.experimental.pallas import tpu as pltpu
from jax.sharding import PartitionSpec as P

NLAT = 24
NEAR_LAT = 8
REGIONS = 64
FAR = 8


HIGHEST = lax.Precision.HIGHEST


def harmonic_tables(grid_lat, degree_count):
    longitudes = 2 * grid_lat
    full_longitudes = 2 * degree_count
    colatitude = (np.arange(grid_lat, dtype=np.float64) + 0.5) * (math.pi / grid_lat)
    cosine = np.cos(colatitude)
    values = [np.ones_like(cosine), cosine]
    for degree in range(2, degree_count):
        values.append(((2 * degree - 1) * cosine * values[-1] - (degree - 1) * values[-2]) / degree)
    degrees = np.arange(degree_count, dtype=np.float64)
    legendre = np.stack(values[:degree_count], axis=1) * np.sqrt((2.0 * degrees + 1.0) / 2.0)
    azimuth = np.arange(longitudes, dtype=np.float64) * (2.0 * math.pi / longitudes)
    halfway = degree_count // 2
    mode_index = np.arange(degree_count, dtype=np.float64)
    frequency = np.where(mode_index < halfway, mode_index, mode_index - halfway + 1.0)
    phases = azimuth[:, None] * frequency[None, :]
    fourier = np.where(mode_index[None, :] < halfway, np.cos(phases), np.sin(phases))
    fourier = fourier * np.where(
        mode_index[None, :] == 0, math.sqrt(1.0 / full_longitudes), math.sqrt(2.0 / full_longitudes)
    )
    synthesis = np.einsum("jl,km->lmjk", legendre, fourier).reshape(
        degree_count * degree_count, grid_lat * longitudes
    )
    quadrature = np.repeat(np.sin(colatitude) * (math.pi / grid_lat), longitudes)
    degree_scale = np.repeat(1.0 / (2.0 * degrees + 1.0), degree_count)
    return (synthesis, quadrature, degree_scale)


def far_coupling(regions, vesicle_total):
    position = np.arange(regions, dtype=np.float64)
    return 1.0 / ((1.0 + np.abs(position[:, None] - position[None, :])) * math.sqrt(vesicle_total))


GROUP = 8

def gather_pair_kernel(t_stride, s_stride, live_ref, tidx_ref, sidx_ref, *refs):
    t_ref, s_ref, o_ref, order_ref, tile_ref, cot_ref = refs
    pairs = live_ref.shape[0]
    scale = 1.0 / math.sqrt(t_ref.shape[1])
    o_ref[...] = jnp.zeros(o_ref.shape, o_ref.dtype)
    cot_ref[...] = jnp.zeros(cot_ref.shape, cot_ref.dtype)

    def pack(p, count):
        order_ref[count] = p
        return count + live_ref[p]

    count = lax.fori_loop(0, pairs, pack, 0, unroll=8)
    for j in range(GROUP):
        order_ref[count + j] = order_ref[0]

    def group_body(g, carry):
        picked = [order_ref[g * GROUP + j] for j in range(GROUP)]
        for j in range(GROUP):
            t_row = (picked[j] if tidx_ref is None else tidx_ref[picked[j]]) * t_stride
            s_row = sidx_ref[picked[j]] * s_stride
            for c in range(3):
                tile_ref[c, pl.ds(j, 1), :] = t_ref[pl.ds(t_row + c, 1), :]
                cot_ref[j, pl.ds(c, 1), :] = t_ref[pl.ds(t_row + 3 + c, 1), :]
                tile_ref[3 + c, pl.ds(j, 1), :] = s_ref[pl.ds(s_row + c, 1), :]
        t_cols = [tile_ref[c].T for c in range(3)]
        s_rows = [tile_ref[3 + c] for c in range(3)]
        for p in range(GROUP):
            distance = None
            for c in range(3):
                apart = t_cols[c][:, p : p + 1] - s_rows[c][p : p + 1, :]
                distance = apart * apart if distance is None else distance + apart * apart
            kernel_block = 1.0 / (1.0 + distance)
            terms = jnp.dot(
                cot_ref[p], kernel_block, precision=HIGHEST, preferred_element_type=jnp.float32
            )
            for c in range(3):
                o_ref[c, pl.ds(picked[p], 1), :] = terms[c : c + 1, :] * scale
        return carry

    lax.fori_loop(0, (count + GROUP - 1) // GROUP, group_body, 0)


def gather_pair_terms(live, target_index, source_index, target_rows, t_stride, source_rows, s_stride):
    pairs = live.shape[0]
    points = target_rows.shape[1]
    vmem = pl.BlockSpec(memory_space=pltpu.VMEM)
    smem = pl.BlockSpec(memory_space=pltpu.SMEM)
    kernel = functools.partial(gather_pair_kernel, t_stride, s_stride)
    if target_index is None:
        indices = (live, source_index)
        body = lambda live_ref, sidx_ref, *refs: kernel(live_ref, None, sidx_ref, *refs)
    else:
        indices = (live, target_index, source_index)
        body = kernel
    return pl.pallas_call(
        body,
        in_specs=[smem] * len(indices) + [vmem, vmem],
        out_specs=vmem,
        out_shape=jax.ShapeDtypeStruct((3, pairs, points), jnp.float32),
        scratch_shapes=[
            pltpu.SMEM((pairs + GROUP,), jnp.int32),
            pltpu.VMEM((6, GROUP, points), jnp.float32),
            pltpu.VMEM((GROUP, 8, points), jnp.float32),
        ],
        name="gather_pair_terms",
    )(*indices, target_rows, source_rows)


def onehot(index, count):
    return (index[:, None] == jnp.arange(count, dtype=jnp.int32)[None, :]).astype(jnp.float32)


def on_device(
    cotangent, surface, region_id, local_target, local_shift, near_target, near_source, near_count
):
    vesicles = cotangent.shape[0]
    coef_count = cotangent.shape[2]
    devices = lax.axis_size("dev")
    slot_count = near_target.shape[2]
    pair_slots = devices * slot_count

    synthesis, quadrature, degree_scale = harmonic_tables(NLAT, NLAT)
    near_synthesis, near_quadrature, unused_scale = harmonic_tables(NEAR_LAT, NLAT)
    points = synthesis.shape[1]
    near_points = near_synthesis.shape[1]
    full = jnp.asarray(synthesis.astype(np.float32))
    near = jnp.asarray(near_synthesis.astype(np.float32))
    contract_rows = (((0,), (0,)), ((), ()))
    cot_flat = cotangent.reshape(vesicles * 3, coef_count)
    surface_flat = surface.reshape(vesicles * 3, coef_count)

    near_cot = jnp.dot(cot_flat, near, precision=HIGHEST).reshape(vesicles, 3, near_points)
    near_shape = jnp.dot(surface_flat, near, precision=HIGHEST).reshape(vesicles, 3, near_points)
    cot_points = jnp.dot(cot_flat, full, precision=HIGHEST).reshape(vesicles, 3, points)
    shape_points = jnp.dot(surface_flat, full, precision=HIGHEST).reshape(vesicles, 3, points)
    stretch = 1.0 / (1.0 + jnp.sum(shape_points * shape_points, axis=1))
    point_total = stretch[:, None, :] * cot_points * jnp.asarray(quadrature.astype(np.float32))
    contract_points = (((1,), (1,)), ((), ()))
    point_coefs = lax.dot_general(
        point_total.reshape(vesicles * 3, points), full, contract_points, precision=HIGHEST
    )
    gradient = lax.optimization_barrier(
        jnp.asarray(degree_scale.astype(np.float32)) * cotangent
        + point_coefs.reshape(cotangent.shape)
    )

    near_vkx = jnp.concatenate([near_shape, near_cot], axis=1)
    rows_per_vesicle = near_vkx.shape[1]
    near_flat = near_vkx.reshape(vesicles * rows_per_vesicle, near_points)

    targets = near_target[0].reshape(pair_slots)
    alive = (
        jnp.arange(slot_count, dtype=jnp.int32)[None, :] < near_count[0][:, None]
    ).reshape(pair_slots)
    picked = jnp.einsum("pv,vkx->pkx", onehot(targets, vesicles), near_vkx, precision=HIGHEST)
    kind = jnp.arange(rows_per_vesicle, dtype=jnp.int32)[None, :, None]
    picked = jnp.where((kind < 3) | alive[:, None, None], picked, 0.0)
    member = onehot(region_id, REGIONS)
    partial_far = lax.dot_general(
        member, cot_flat.reshape(vesicles, 3 * coef_count), contract_rows, precision=HIGHEST
    ).reshape(REGIONS, 3, coef_count)[:, :, :FAR].reshape(REGIONS, 3 * FAR)
    far_rows = REGIONS * 3 * FAR // (slot_count * near_points)
    far_block = partial_far.reshape(1, slot_count, far_rows, near_points)
    far_block = jnp.broadcast_to(far_block, (devices, slot_count, far_rows, near_points))
    pair_rows = rows_per_vesicle + far_rows
    outgoing = jnp.concatenate(
        [picked, far_block.reshape(pair_slots, far_rows, near_points)], axis=1
    ).reshape(pair_slots * pair_rows, near_points)
    incoming = lax.all_to_all(outgoing, "dev", split_axis=0, concat_axis=0, tiled=True)
    peer_rows = jnp.sum(incoming.reshape(devices, slot_count * pair_rows, near_points), axis=0)
    far_total = peer_rows.reshape(slot_count, pair_rows, near_points)[:, rows_per_vesicle:, :]
    far_total = far_total.reshape(REGIONS, 3 * FAR)
    sources = jnp.clip(near_source[0].reshape(pair_slots), 0, vesicles - 1)
    source_onehot = onehot(sources, vesicles)

    local_target = jnp.clip(local_target, 0, vesicles - 1)
    local_source = (local_target + local_shift) % vesicles
    local_onehot = onehot(local_source, vesicles)
    local_terms = gather_pair_terms(
        jnp.ones((vesicles,), jnp.int32),
        local_target,
        local_source,
        near_flat,
        rows_per_vesicle,
        near_flat,
        rows_per_vesicle,
    )
    cot_size = jnp.max(
        jnp.stack([jnp.abs(incoming[3 + c :: pair_rows]) for c in range(3)]), axis=(0, 2)
    )
    live = (cot_size > 0.0).astype(jnp.int32)
    remote_terms = gather_pair_terms(
        live,
        None,
        sources,
        incoming,
        pair_rows,
        near_flat,
        rows_per_vesicle,
    )
    near_total = jnp.einsum(
        "pv,kpx->vkx", local_onehot, local_terms, precision=HIGHEST
    ) + jnp.einsum("pv,kpx->vkx", source_onehot, remote_terms, precision=HIGHEST)

    near_weighted = near_total.reshape(vesicles * 3, near_points) * jnp.asarray(
        near_quadrature.astype(np.float32)
    )
    gradient = gradient + lax.dot_general(
        near_weighted, near, contract_points, precision=HIGHEST
    ).reshape(cotangent.shape)

    coupling = jnp.asarray(far_coupling(REGIONS, vesicles * devices).astype(np.float32))
    far_field = lax.dot_general(coupling, far_total, contract_rows, precision=HIGHEST)
    far_terms = jnp.dot(member, far_field, precision=HIGHEST).reshape(vesicles, 3, FAR)
    return gradient + jnp.pad(far_terms, ((0, 0), (0, 0), (0, coef_count - FAR)))


def solution(mesh):
    in_specs = (
        P("dev", None, None),
        P("dev", None, None),
        P("dev"),
        P("dev"),
        P("dev"),
        P("dev", None, None),
        P("dev", None, None),
        P("dev", None),
    )
    out_specs = P("dev", None, None)
    return jax.shard_map(
        on_device, mesh=mesh, in_specs=in_specs, out_specs=out_specs, check_vma=False
    )
```

```python
import functools
import math

import jax
import jax.numpy as jnp
import numpy as np
from jax import lax
from jax.experimental import pallas as pl
from jax.experimental.pallas import tpu as pltpu
from jax.sharding import PartitionSpec as P

NLAT = 24
NEAR_LAT = 8
REGIONS = 64
FAR = 8


HIGHEST = lax.Precision.HIGHEST


def harmonic_tables(grid_lat, degree_count):
    longitudes = 2 * grid_lat
    full_longitudes = 2 * degree_count
    colatitude = (np.arange(grid_lat, dtype=np.float64) + 0.5) * (math.pi / grid_lat)
    cosine = np.cos(colatitude)
    values = [np.ones_like(cosine), cosine]
    for degree in range(2, degree_count):
        values.append(((2 * degree - 1) * cosine * values[-1] - (degree - 1) * values[-2]) / degree)
    degrees = np.arange(degree_count, dtype=np.float64)
    legendre = np.stack(values[:degree_count], axis=1) * np.sqrt((2.0 * degrees + 1.0) / 2.0)
    azimuth = np.arange(longitudes, dtype=np.float64) * (2.0 * math.pi / longitudes)
    halfway = degree_count // 2
    mode_index = np.arange(degree_count, dtype=np.float64)
    frequency = np.where(mode_index < halfway, mode_index, mode_index - halfway + 1.0)
    phases = azimuth[:, None] * frequency[None, :]
    fourier = np.where(mode_index[None, :] < halfway, np.cos(phases), np.sin(phases))
    fourier = fourier * np.where(
        mode_index[None, :] == 0, math.sqrt(1.0 / full_longitudes), math.sqrt(2.0 / full_longitudes)
    )
    synthesis = np.einsum("jl,km->lmjk", legendre, fourier).reshape(
        degree_count * degree_count, grid_lat * longitudes
    )
    quadrature = np.repeat(np.sin(colatitude) * (math.pi / grid_lat), longitudes)
    degree_scale = np.repeat(1.0 / (2.0 * degrees + 1.0), degree_count)
    return (synthesis, quadrature, degree_scale)


def far_coupling(regions, vesicle_total):
    position = np.arange(regions, dtype=np.float64)
    return 1.0 / ((1.0 + np.abs(position[:, None] - position[None, :])) * math.sqrt(vesicle_total))


GROUP = 8

def gather_pair_kernel(t_stride, s_stride, live_ref, tidx_ref, sidx_ref, *refs):
    t_ref, s_ref, o_ref, order_ref, tile_ref, cot_ref = refs
    pairs = live_ref.shape[0]
    scale = 1.0 / math.sqrt(t_ref.shape[1])
    o_ref[...] = jnp.zeros(o_ref.shape, o_ref.dtype)
    cot_ref[...] = jnp.zeros(cot_ref.shape, cot_ref.dtype)

    def pack(p, count):
        order_ref[count] = p
        return count + live_ref[p]

    count = lax.fori_loop(0, pairs, pack, 0, unroll=8)
    for j in range(GROUP):
        order_ref[count + j] = order_ref[0]

    def group_body(g, carry):
        picked = [order_ref[g * GROUP + j] for j in range(GROUP)]
        for j in range(GROUP):
            t_row = (picked[j] if tidx_ref is None else tidx_ref[picked[j]]) * t_stride
            s_row = sidx_ref[picked[j]] * s_stride
            for c in range(3):
                tile_ref[c, pl.ds(j, 1), :] = t_ref[pl.ds(t_row + c, 1), :]
                cot_ref[j, pl.ds(c, 1), :] = t_ref[pl.ds(t_row + 3 + c, 1), :]
                tile_ref[3 + c, pl.ds(j, 1), :] = s_ref[pl.ds(s_row + c, 1), :]
        t_cols = [tile_ref[c].T for c in range(3)]
        s_rows = [tile_ref[3 + c] for c in range(3)]
        for p in range(GROUP):
            distance = None
            for c in range(3):
                apart = t_cols[c][:, p : p + 1] - s_rows[c][p : p + 1, :]
                distance = apart * apart if distance is None else distance + apart * apart
            kernel_block = 1.0 / (1.0 + distance)
            terms = jnp.dot(
                cot_ref[p], kernel_block, precision=HIGHEST, preferred_element_type=jnp.float32
            )
            for c in range(3):
                o_ref[c, pl.ds(picked[p], 1), :] = terms[c : c + 1, :] * scale
        return carry

    lax.fori_loop(0, (count + GROUP - 1) // GROUP, group_body, 0)


def gather_pair_terms(live, target_index, source_index, target_rows, t_stride, source_rows, s_stride):
    pairs = live.shape[0]
    points = target_rows.shape[1]
    vmem = pl.BlockSpec(memory_space=pltpu.VMEM)
    smem = pl.BlockSpec(memory_space=pltpu.SMEM)
    kernel = functools.partial(gather_pair_kernel, t_stride, s_stride)
    if target_index is None:
        indices = (live, source_index)
        body = lambda live_ref, sidx_ref, *refs: kernel(live_ref, None, sidx_ref, *refs)
    else:
        indices = (live, target_index, source_index)
        body = kernel
    return pl.pallas_call(
        body,
        in_specs=[smem] * len(indices) + [vmem, vmem],
        out_specs=vmem,
        out_shape=jax.ShapeDtypeStruct((3, pairs, points), jnp.float32),
        scratch_shapes=[
            pltpu.SMEM((pairs + GROUP,), jnp.int32),
            pltpu.VMEM((6, GROUP, points), jnp.float32),
            pltpu.VMEM((GROUP, 8, points), jnp.float32),
        ],
        name="gather_pair_terms",
    )(*indices, target_rows, source_rows)


def onehot(index, count):
    return (index[:, None] == jnp.arange(count, dtype=jnp.int32)[None, :]).astype(jnp.float32)


def on_device(
    cotangent, surface, region_id, local_target, local_shift, near_target, near_source, near_count
):
    vesicles = cotangent.shape[0]
    coef_count = cotangent.shape[2]
    devices = lax.axis_size("dev")
    slot_count = near_target.shape[2]
    pair_slots = devices * slot_count

    synthesis, quadrature, degree_scale = harmonic_tables(NLAT, NLAT)
    near_synthesis, near_quadrature, unused_scale = harmonic_tables(NEAR_LAT, NLAT)
    points = synthesis.shape[1]
    near_points = near_synthesis.shape[1]
    full = jnp.asarray(synthesis.astype(np.float32))
    near = jnp.asarray(near_synthesis.astype(np.float32))
    contract_rows = (((0,), (0,)), ((), ()))
    cot_flat = cotangent.reshape(vesicles * 3, coef_count)
    surface_flat = surface.reshape(vesicles * 3, coef_count)

    near_cot = jnp.dot(cot_flat, near, precision=HIGHEST).reshape(vesicles, 3, near_points)
    near_shape = jnp.dot(surface_flat, near, precision=HIGHEST).reshape(vesicles, 3, near_points)
    cot_points = jnp.dot(cot_flat, full, precision=HIGHEST).reshape(vesicles, 3, points)
    shape_points = jnp.dot(surface_flat, full, precision=HIGHEST).reshape(vesicles, 3, points)
    stretch = 1.0 / (1.0 + jnp.sum(shape_points * shape_points, axis=1))
    point_total = stretch[:, None, :] * cot_points * jnp.asarray(quadrature.astype(np.float32))
    contract_points = (((1,), (1,)), ((), ()))
    point_coefs = lax.dot_general(
        point_total.reshape(vesicles * 3, points), full, contract_points, precision=HIGHEST
    )
    gradient = lax.optimization_barrier(
        jnp.asarray(degree_scale.astype(np.float32)) * cotangent
        + point_coefs.reshape(cotangent.shape)
    )

    near_vkx = jnp.concatenate([near_shape, near_cot], axis=1)
    rows_per_vesicle = near_vkx.shape[1]
    near_flat = near_vkx.reshape(vesicles * rows_per_vesicle, near_points)

    targets = near_target[0].reshape(pair_slots)
    alive = (
        jnp.arange(slot_count, dtype=jnp.int32)[None, :] < near_count[0][:, None]
    ).reshape(pair_slots)
    picked = jnp.einsum("pv,vkx->pkx", onehot(targets, vesicles), near_vkx, precision=HIGHEST)
    kind = jnp.arange(rows_per_vesicle, dtype=jnp.int32)[None, :, None]
    picked = jnp.where((kind < 3) | alive[:, None, None], picked, 0.0)
    member = onehot(region_id, REGIONS)
    partial_far = lax.dot_general(
        member, cot_flat.reshape(vesicles, 3 * coef_count), contract_rows, precision=HIGHEST
    ).reshape(REGIONS, 3, coef_count)[:, :, :FAR].reshape(REGIONS, 3 * FAR)
    far_rows = REGIONS * 3 * FAR // (slot_count * near_points)
    far_block = partial_far.reshape(1, slot_count, far_rows, near_points)
    far_block = jnp.broadcast_to(far_block, (devices, slot_count, far_rows, near_points))
    pair_rows = rows_per_vesicle + far_rows
    outgoing = jnp.concatenate(
        [picked, far_block.reshape(pair_slots, far_rows, near_points)], axis=1
    ).reshape(pair_slots * pair_rows, near_points)
    incoming = lax.all_to_all(outgoing, "dev", split_axis=0, concat_axis=0, tiled=True)
    peer_rows = jnp.sum(incoming.reshape(devices, slot_count * pair_rows, near_points), axis=0)
    far_total = peer_rows.reshape(slot_count, pair_rows, near_points)[:, rows_per_vesicle:, :]
    far_total = far_total.reshape(REGIONS, 3 * FAR)
    sources = jnp.clip(near_source[0].reshape(pair_slots), 0, vesicles - 1)
    source_onehot = onehot(sources, vesicles)

    local_target = jnp.clip(local_target, 0, vesicles - 1)
    local_source = (local_target + local_shift) % vesicles
    local_onehot = onehot(local_source, vesicles)
    local_terms = gather_pair_terms(
        jnp.ones((vesicles,), jnp.int32),
        local_target,
        local_source,
        near_flat,
        rows_per_vesicle,
        near_flat,
        rows_per_vesicle,
    )
    row_size = jnp.max(jnp.abs(incoming), axis=1).reshape(pair_slots, pair_rows)
    live = (jnp.max(row_size[:, 3:rows_per_vesicle], axis=1) > 0.0).astype(jnp.int32)
    remote_terms = gather_pair_terms(
        live,
        None,
        sources,
        incoming,
        pair_rows,
        near_flat,
        rows_per_vesicle,
    )
    near_total = jnp.einsum(
        "pv,kpx->vkx", local_onehot, local_terms, precision=HIGHEST
    ) + jnp.einsum("pv,kpx->vkx", source_onehot, remote_terms, precision=HIGHEST)

    near_weighted = near_total.reshape(vesicles * 3, near_points) * jnp.asarray(
        near_quadrature.astype(np.float32)
    )
    gradient = gradient + lax.dot_general(
        near_weighted, near, contract_points, precision=HIGHEST
    ).reshape(cotangent.shape)

    coupling = jnp.asarray(far_coupling(REGIONS, vesicles * devices).astype(np.float32))
    far_field = lax.dot_general(coupling, far_total, contract_rows, precision=HIGHEST)
    far_terms = jnp.dot(member, far_field, precision=HIGHEST).reshape(vesicles, 3, FAR)
    return gradient + jnp.pad(far_terms, ((0, 0), (0, 0), (0, coef_count - FAR)))


def solution(mesh):
    in_specs = (
        P("dev", None, None),
        P("dev", None, None),
        P("dev"),
        P("dev"),
        P("dev"),
        P("dev", None, None),
        P("dev", None, None),
        P("dev", None),
    )
    out_specs = P("dev", None, None)
    return jax.shard_map(
        on_device, mesh=mesh, in_specs=in_specs, out_specs=out_specs, check_vma=False
    )
```

```python
import functools
import math

import jax
import jax.numpy as jnp
import numpy as np
from jax import lax
from jax.experimental import pallas as pl
from jax.experimental.pallas import tpu as pltpu
from jax.sharding import PartitionSpec as P

NLAT = 24
NEAR_LAT = 8
REGIONS = 64
FAR = 8


HIGHEST = lax.Precision.HIGHEST


def harmonic_tables(grid_lat, degree_count):
    longitudes = 2 * grid_lat
    full_longitudes = 2 * degree_count
    colatitude = (np.arange(grid_lat, dtype=np.float64) + 0.5) * (math.pi / grid_lat)
    cosine = np.cos(colatitude)
    values = [np.ones_like(cosine), cosine]
    for degree in range(2, degree_count):
        values.append(((2 * degree - 1) * cosine * values[-1] - (degree - 1) * values[-2]) / degree)
    degrees = np.arange(degree_count, dtype=np.float64)
    legendre = np.stack(values[:degree_count], axis=1) * np.sqrt((2.0 * degrees + 1.0) / 2.0)
    azimuth = np.arange(longitudes, dtype=np.float64) * (2.0 * math.pi / longitudes)
    halfway = degree_count // 2
    mode_index = np.arange(degree_count, dtype=np.float64)
    frequency = np.where(mode_index < halfway, mode_index, mode_index - halfway + 1.0)
    phases = azimuth[:, None] * frequency[None, :]
    fourier = np.where(mode_index[None, :] < halfway, np.cos(phases), np.sin(phases))
    fourier = fourier * np.where(
        mode_index[None, :] == 0, math.sqrt(1.0 / full_longitudes), math.sqrt(2.0 / full_longitudes)
    )
    synthesis = np.einsum("jl,km->lmjk", legendre, fourier).reshape(
        degree_count * degree_count, grid_lat * longitudes
    )
    quadrature = np.repeat(np.sin(colatitude) * (math.pi / grid_lat), longitudes)
    degree_scale = np.repeat(1.0 / (2.0 * degrees + 1.0), degree_count)
    return (synthesis, quadrature, degree_scale)


def far_coupling(regions, vesicle_total):
    position = np.arange(regions, dtype=np.float64)
    return 1.0 / ((1.0 + np.abs(position[:, None] - position[None, :])) * math.sqrt(vesicle_total))


GROUP = 8

def gather_pair_kernel(t_stride, s_stride, live_ref, tidx_ref, sidx_ref, *refs):
    t_ref, s_ref, o_ref, order_ref, tile_ref, cot_ref = refs
    pairs = live_ref.shape[0]
    scale = 1.0 / math.sqrt(t_ref.shape[1])
    o_ref[...] = jnp.zeros(o_ref.shape, o_ref.dtype)
    cot_ref[...] = jnp.zeros(cot_ref.shape, cot_ref.dtype)

    def pack(p, count):
        order_ref[count] = p
        return count + live_ref[p]

    count = lax.fori_loop(0, pairs, pack, 0, unroll=8)
    for j in range(GROUP):
        order_ref[count + j] = order_ref[0]

    def group_body(g, carry):
        picked = [order_ref[g * GROUP + j] for j in range(GROUP)]
        for j in range(GROUP):
            t_row = (picked[j] if tidx_ref is None else tidx_ref[picked[j]]) * t_stride
            s_row = sidx_ref[picked[j]] * s_stride
            for c in range(3):
                tile_ref[c, pl.ds(j, 1), :] = t_ref[pl.ds(t_row + c, 1), :]
                cot_ref[j, pl.ds(c, 1), :] = t_ref[pl.ds(t_row + 3 + c, 1), :]
                tile_ref[3 + c, pl.ds(j, 1), :] = s_ref[pl.ds(s_row + c, 1), :]
        t_cols = [tile_ref[c].T for c in range(3)]
        s_rows = [tile_ref[3 + c] for c in range(3)]
        for p in range(GROUP):
            distance = None
            for c in range(3):
                apart = t_cols[c][:, p : p + 1] - s_rows[c][p : p + 1, :]
                distance = apart * apart if distance is None else distance + apart * apart
            kernel_block = 1.0 / (1.0 + distance)
            terms = jnp.dot(
                cot_ref[p], kernel_block, precision=HIGHEST, preferred_element_type=jnp.float32
            )
            for c in range(3):
                o_ref[c, pl.ds(picked[p], 1), :] = terms[c : c + 1, :] * scale
        return carry

    lax.fori_loop(0, (count + GROUP - 1) // GROUP, group_body, 0)


def gather_pair_terms(live, target_index, source_index, target_rows, t_stride, source_rows, s_stride):
    pairs = live.shape[0]
    points = target_rows.shape[1]
    vmem = pl.BlockSpec(memory_space=pltpu.VMEM)
    smem = pl.BlockSpec(memory_space=pltpu.SMEM)
    kernel = functools.partial(gather_pair_kernel, t_stride, s_stride)
    if target_index is None:
        indices = (live, source_index)
        body = lambda live_ref, sidx_ref, *refs: kernel(live_ref, None, sidx_ref, *refs)
    else:
        indices = (live, target_index, source_index)
        body = kernel
    return pl.pallas_call(
        body,
        in_specs=[smem] * len(indices) + [vmem, vmem],
        out_specs=vmem,
        out_shape=jax.ShapeDtypeStruct((3, pairs, points), jnp.float32),
        scratch_shapes=[
            pltpu.SMEM((pairs + GROUP,), jnp.int32),
            pltpu.VMEM((6, GROUP, points), jnp.float32),
            pltpu.VMEM((GROUP, 8, points), jnp.float32),
        ],
        name="gather_pair_terms",
    )(*indices, target_rows, source_rows)


def onehot(index, count):
    return (index[:, None] == jnp.arange(count, dtype=jnp.int32)[None, :]).astype(jnp.float32)


def on_device(
    cotangent, surface, region_id, local_target, local_shift, near_target, near_source, near_count
):
    vesicles = cotangent.shape[0]
    coef_count = cotangent.shape[2]
    devices = lax.axis_size("dev")
    slot_count = near_target.shape[2]
    pair_slots = devices * slot_count

    synthesis, quadrature, degree_scale = harmonic_tables(NLAT, NLAT)
    near_synthesis, near_quadrature, unused_scale = harmonic_tables(NEAR_LAT, NLAT)
    points = synthesis.shape[1]
    near_points = near_synthesis.shape[1]
    full = jnp.asarray(synthesis.astype(np.float32))
    near = jnp.asarray(near_synthesis.astype(np.float32))
    contract_rows = (((0,), (0,)), ((), ()))
    cot_flat = cotangent.reshape(vesicles * 3, coef_count)
    surface_flat = surface.reshape(vesicles * 3, coef_count)

    near_cot = jnp.dot(cot_flat, near, precision=HIGHEST).reshape(vesicles, 3, near_points)
    near_shape = jnp.dot(surface_flat, near, precision=HIGHEST).reshape(vesicles, 3, near_points)
    cot_points = jnp.dot(cot_flat, full, precision=HIGHEST).reshape(vesicles, 3, points)
    shape_points = jnp.dot(surface_flat, full, precision=HIGHEST).reshape(vesicles, 3, points)
    stretch = 1.0 / (1.0 + jnp.sum(shape_points * shape_points, axis=1))
    point_total = stretch[:, None, :] * cot_points * jnp.asarray(quadrature.astype(np.float32))
    contract_points = (((1,), (1,)), ((), ()))
    point_coefs = lax.dot_general(
        point_total.reshape(vesicles * 3, points), full, contract_points, precision=HIGHEST
    )
    gradient = lax.optimization_barrier(
        jnp.asarray(degree_scale.astype(np.float32)) * cotangent
        + point_coefs.reshape(cotangent.shape)
    )

    near_vkx = jnp.concatenate([near_shape, near_cot], axis=1)
    rows_per_vesicle = near_vkx.shape[1]
    near_flat = near_vkx.reshape(vesicles * rows_per_vesicle, near_points)

    tile = 8
    member = onehot(region_id, REGIONS)
    partial_far = lax.dot_general(
        member, cot_flat.reshape(vesicles, 3 * coef_count), contract_rows, precision=HIGHEST
    ).reshape(REGIONS, 3, coef_count)[:, :, :FAR].reshape(-1, near_points)
    spare = tile - rows_per_vesicle
    far_count = partial_far.shape[0]
    far_tiles = -(-(far_count - slot_count * spare) // tile)
    partial_far = jnp.pad(
        partial_far, ((0, slot_count * spare + far_tiles * tile - far_count), (0, 0))
    )
    kind = jnp.arange(rows_per_vesicle, dtype=jnp.int32)[None, :, None]
    pieces = []
    for slot in range(slot_count):
        alive = slot < near_count[0]
        picked = jnp.einsum(
            "qv,vkx->qkx", onehot(near_target[0, :, slot], vesicles), near_vkx, precision=HIGHEST
        )
        picked = jnp.where((kind < 3) | alive[:, None, None], picked, 0.0)
        far_part = partial_far[slot * spare : (slot + 1) * spare]
        pieces += [picked, jnp.broadcast_to(far_part[None], (devices, spare, near_points))]
    far_rest = partial_far[slot_count * spare :]
    pieces.append(jnp.broadcast_to(far_rest[None], (devices,) + far_rest.shape))
    outgoing = jnp.concatenate(pieces, axis=1)
    peer_tiles = outgoing.shape[1] // tile
    incoming = lax.all_to_all(outgoing, "dev", split_axis=0, concat_axis=0, tiled=True)
    peer_rows = jnp.sum(incoming, axis=0)
    far_total = jnp.concatenate(
        [peer_rows[slot * tile + rows_per_vesicle : (slot + 1) * tile] for slot in range(slot_count)]
        + [peer_rows[slot_count * tile :]]
    )[:far_count].reshape(REGIONS, 3 * FAR)
    row_size = jnp.max(jnp.abs(incoming), axis=2)
    live = jnp.stack(
        [
            jnp.max(row_size[:, slot * tile + 3 : slot * tile + rows_per_vesicle], axis=1)
            for slot in range(slot_count)
        ],
        axis=1,
    ).reshape(pair_slots)
    live = (live > 0.0).astype(jnp.int32)
    incoming = incoming.reshape(devices * peer_tiles * tile, near_points)
    pair_tile = np.arange(pair_slots) // slot_count * peer_tiles + np.arange(pair_slots) % slot_count
    sources = jnp.clip(near_source[0].reshape(pair_slots), 0, vesicles - 1)
    source_onehot = onehot(sources, vesicles)

    local_target = jnp.clip(local_target, 0, vesicles - 1)
    local_source = (local_target + local_shift) % vesicles
    local_onehot = onehot(local_source, vesicles)
    local_terms = gather_pair_terms(
        jnp.ones((vesicles,), jnp.int32),
        local_target,
        local_source,
        near_flat,
        rows_per_vesicle,
        near_flat,
        rows_per_vesicle,
    )
    remote_terms = gather_pair_terms(
        live,
        jnp.asarray(pair_tile.astype(np.int32)),
        sources,
        incoming,
        tile,
        near_flat,
        rows_per_vesicle,
    )
    near_total = jnp.einsum(
        "pv,kpx->vkx", local_onehot, local_terms, precision=HIGHEST
    ) + jnp.einsum("pv,kpx->vkx", source_onehot, remote_terms, precision=HIGHEST)

    near_weighted = near_total.reshape(vesicles * 3, near_points) * jnp.asarray(
        near_quadrature.astype(np.float32)
    )
    gradient = gradient + lax.dot_general(
        near_weighted, near, contract_points, precision=HIGHEST
    ).reshape(cotangent.shape)

    coupling = jnp.asarray(far_coupling(REGIONS, vesicles * devices).astype(np.float32))
    far_field = lax.dot_general(coupling, far_total, contract_rows, precision=HIGHEST)
    far_terms = jnp.dot(member, far_field, precision=HIGHEST).reshape(vesicles, 3, FAR)
    return gradient + jnp.pad(far_terms, ((0, 0), (0, 0), (0, coef_count - FAR)))


def solution(mesh):
    in_specs = (
        P("dev", None, None),
        P("dev", None, None),
        P("dev"),
        P("dev"),
        P("dev"),
        P("dev", None, None),
        P("dev", None, None),
        P("dev", None),
    )
    out_specs = P("dev", None, None)
    return jax.shard_map(
        on_device, mesh=mesh, in_specs=in_specs, out_specs=out_specs, check_vma=False
    )
```

```python
import functools
import math

import jax
import jax.numpy as jnp
import numpy as np
from jax import lax
from jax.experimental import pallas as pl
from jax.experimental.pallas import tpu as pltpu
from jax.sharding import PartitionSpec as P

NLAT = 24
NEAR_LAT = 8
REGIONS = 64
FAR = 8


HIGHEST = lax.Precision.HIGHEST


def harmonic_tables(grid_lat, degree_count):
    longitudes = 2 * grid_lat
    full_longitudes = 2 * degree_count
    colatitude = (np.arange(grid_lat, dtype=np.float64) + 0.5) * (math.pi / grid_lat)
    cosine = np.cos(colatitude)
    values = [np.ones_like(cosine), cosine]
    for degree in range(2, degree_count):
        values.append(((2 * degree - 1) * cosine * values[-1] - (degree - 1) * values[-2]) / degree)
    degrees = np.arange(degree_count, dtype=np.float64)
    legendre = np.stack(values[:degree_count], axis=1) * np.sqrt((2.0 * degrees + 1.0) / 2.0)
    azimuth = np.arange(longitudes, dtype=np.float64) * (2.0 * math.pi / longitudes)
    halfway = degree_count // 2
    mode_index = np.arange(degree_count, dtype=np.float64)
    frequency = np.where(mode_index < halfway, mode_index, mode_index - halfway + 1.0)
    phases = azimuth[:, None] * frequency[None, :]
    fourier = np.where(mode_index[None, :] < halfway, np.cos(phases), np.sin(phases))
    fourier = fourier * np.where(
        mode_index[None, :] == 0, math.sqrt(1.0 / full_longitudes), math.sqrt(2.0 / full_longitudes)
    )
    synthesis = np.einsum("jl,km->lmjk", legendre, fourier).reshape(
        degree_count * degree_count, grid_lat * longitudes
    )
    quadrature = np.repeat(np.sin(colatitude) * (math.pi / grid_lat), longitudes)
    degree_scale = np.repeat(1.0 / (2.0 * degrees + 1.0), degree_count)
    return (synthesis, quadrature, degree_scale)


def far_coupling(regions, vesicle_total):
    position = np.arange(regions, dtype=np.float64)
    return 1.0 / ((1.0 + np.abs(position[:, None] - position[None, :])) * math.sqrt(vesicle_total))


GROUP = 8

def gather_pair_kernel(t_stride, s_stride, live_ref, tidx_ref, sidx_ref, *refs):
    t_ref, s_ref, o_ref, order_ref, tile_ref, cot_ref = refs
    pairs = live_ref.shape[0] * live_ref.shape[1]
    scale = 1.0 / math.sqrt(t_ref.shape[1])
    o_ref[...] = jnp.zeros(o_ref.shape, o_ref.dtype)
    cot_ref[...] = jnp.zeros(cot_ref.shape, cot_ref.dtype)

    width = live_ref.shape[1]

    def pack(p, count):
        order_ref[count] = p
        return count + live_ref[p // width, p % width]

    count = lax.fori_loop(0, pairs, pack, 0, unroll=8)
    for j in range(GROUP):
        order_ref[count + j] = order_ref[0]

    def group_body(g, carry):
        picked = [order_ref[g * GROUP + j] for j in range(GROUP)]
        for j in range(GROUP):
            t_row = (picked[j] if tidx_ref is None else tidx_ref[picked[j]]) * t_stride
            s_row = sidx_ref[picked[j]] * s_stride
            for c in range(3):
                tile_ref[c, pl.ds(j, 1), :] = t_ref[pl.ds(t_row + c, 1), :]
                cot_ref[j, pl.ds(c, 1), :] = t_ref[pl.ds(t_row + 3 + c, 1), :]
                tile_ref[3 + c, pl.ds(j, 1), :] = s_ref[pl.ds(s_row + c, 1), :]
        t_cols = [tile_ref[c].T for c in range(3)]
        s_rows = [tile_ref[3 + c] for c in range(3)]
        for p in range(GROUP):
            distance = None
            for c in range(3):
                apart = t_cols[c][:, p : p + 1] - s_rows[c][p : p + 1, :]
                distance = apart * apart if distance is None else distance + apart * apart
            kernel_block = 1.0 / (1.0 + distance)
            terms = jnp.dot(
                cot_ref[p], kernel_block, precision=HIGHEST, preferred_element_type=jnp.float32
            )
            for c in range(3):
                o_ref[c, pl.ds(picked[p], 1), :] = terms[c : c + 1, :] * scale
        return carry

    lax.fori_loop(0, (count + GROUP - 1) // GROUP, group_body, 0)


def gather_pair_terms(live, target_index, source_index, target_rows, t_stride, source_rows, s_stride):
    pairs = live.shape[0] * live.shape[1]
    points = target_rows.shape[1]
    vmem = pl.BlockSpec(memory_space=pltpu.VMEM)
    smem = pl.BlockSpec(memory_space=pltpu.SMEM)
    kernel = functools.partial(gather_pair_kernel, t_stride, s_stride)
    if target_index is None:
        indices = (live, source_index)
        body = lambda live_ref, sidx_ref, *refs: kernel(live_ref, None, sidx_ref, *refs)
    else:
        indices = (live, target_index, source_index)
        body = kernel
    return pl.pallas_call(
        body,
        in_specs=[smem] * len(indices) + [vmem, vmem],
        out_specs=vmem,
        out_shape=jax.ShapeDtypeStruct((3, pairs, points), jnp.float32),
        scratch_shapes=[
            pltpu.SMEM((pairs + GROUP,), jnp.int32),
            pltpu.VMEM((6, GROUP, points), jnp.float32),
            pltpu.VMEM((GROUP, 8, points), jnp.float32),
        ],
        name="gather_pair_terms",
    )(*indices, target_rows, source_rows)


def onehot(index, count):
    return (index[:, None] == jnp.arange(count, dtype=jnp.int32)[None, :]).astype(jnp.float32)


def on_device(
    cotangent, surface, region_id, local_target, local_shift, near_target, near_source, near_count
):
    vesicles = cotangent.shape[0]
    coef_count = cotangent.shape[2]
    devices = lax.axis_size("dev")
    slot_count = near_target.shape[2]
    pair_slots = devices * slot_count

    synthesis, quadrature, degree_scale = harmonic_tables(NLAT, NLAT)
    near_synthesis, near_quadrature, unused_scale = harmonic_tables(NEAR_LAT, NLAT)
    points = synthesis.shape[1]
    near_points = near_synthesis.shape[1]
    full = jnp.asarray(synthesis.astype(np.float32))
    near = jnp.asarray(near_synthesis.astype(np.float32))
    contract_rows = (((0,), (0,)), ((), ()))
    cot_flat = cotangent.reshape(vesicles * 3, coef_count)
    surface_flat = surface.reshape(vesicles * 3, coef_count)

    near_cot = jnp.dot(cot_flat, near, precision=HIGHEST).reshape(vesicles, 3, near_points)
    near_shape = jnp.dot(surface_flat, near, precision=HIGHEST).reshape(vesicles, 3, near_points)
    cot_points = jnp.dot(cot_flat, full, precision=HIGHEST).reshape(vesicles, 3, points)
    shape_points = jnp.dot(surface_flat, full, precision=HIGHEST).reshape(vesicles, 3, points)
    stretch = 1.0 / (1.0 + jnp.sum(shape_points * shape_points, axis=1))
    point_total = stretch[:, None, :] * cot_points * jnp.asarray(quadrature.astype(np.float32))
    contract_points = (((1,), (1,)), ((), ()))
    point_coefs = lax.dot_general(
        point_total.reshape(vesicles * 3, points), full, contract_points, precision=HIGHEST
    )
    gradient = lax.optimization_barrier(
        jnp.asarray(degree_scale.astype(np.float32)) * cotangent
        + point_coefs.reshape(cotangent.shape)
    )

    near_vkx = jnp.concatenate([near_shape, near_cot], axis=1)
    rows_per_vesicle = near_vkx.shape[1]
    near_flat = near_vkx.reshape(vesicles * rows_per_vesicle, near_points)

    tile = 8
    member = onehot(region_id, REGIONS)
    partial_far = lax.dot_general(
        member, cot_flat.reshape(vesicles, 3 * coef_count), contract_rows, precision=HIGHEST
    ).reshape(REGIONS, 3, coef_count)[:, :, :FAR].reshape(-1, near_points)
    spare = tile - rows_per_vesicle
    far_count = partial_far.shape[0]
    far_tiles = -(-(far_count - slot_count * spare) // tile)
    partial_far = jnp.pad(
        partial_far, ((0, slot_count * spare + far_tiles * tile - far_count), (0, 0))
    )
    near_tiles = jnp.pad(near_vkx, ((0, 0), (0, spare), (0, 0)))
    peer_tiles = slot_count + far_tiles
    wanted = jnp.pad(near_target[0], ((0, 0), (0, far_tiles)), constant_values=-1)
    outgoing = jnp.einsum(
        "qsv,vkx->qskx",
        (wanted[:, :, None] == jnp.arange(vesicles, dtype=jnp.int32)).astype(jnp.float32),
        near_tiles,
        precision=HIGHEST,
    )
    kind = jnp.arange(tile, dtype=jnp.int32)[None, None, :, None]
    alive = jnp.pad(
        jnp.arange(slot_count, dtype=jnp.int32)[None, :] < near_count[0][:, None],
        ((0, 0), (0, far_tiles)),
    )
    outgoing = jnp.where((kind < 3) | alive[:, :, None, None], outgoing, 0.0)
    far_add = jnp.concatenate(
        [
            jnp.pad(partial_far[slot * spare : (slot + 1) * spare], ((rows_per_vesicle, 0), (0, 0)))
            for slot in range(slot_count)
        ]
        + [partial_far[slot_count * spare :]]
    ).reshape(peer_tiles, tile, near_points)
    outgoing = (outgoing + far_add[None]).reshape(devices, peer_tiles * tile, near_points)
    incoming = lax.all_to_all(outgoing, "dev", split_axis=0, concat_axis=0, tiled=True)
    peer_rows = jnp.sum(incoming, axis=0)
    far_total = jnp.concatenate(
        [peer_rows[slot * tile + rows_per_vesicle : (slot + 1) * tile] for slot in range(slot_count)]
        + [peer_rows[slot_count * tile :]]
    )[:far_count].reshape(REGIONS, 3 * FAR)
    row_size = jnp.max(jnp.abs(incoming), axis=2)
    live = jnp.stack(
        [
            jnp.max(row_size[:, slot * tile + 3 : slot * tile + rows_per_vesicle], axis=1)
            for slot in range(slot_count)
        ],
        axis=1,
    )
    live = (live > 0.0).astype(jnp.int32)
    incoming = incoming.reshape(devices * peer_tiles * tile, near_points)
    pair_tile = np.arange(pair_slots) // slot_count * peer_tiles + np.arange(pair_slots) % slot_count
    sources = jnp.clip(near_source[0].reshape(pair_slots), 0, vesicles - 1)
    source_onehot = onehot(sources, vesicles)

    local_target = jnp.clip(local_target, 0, vesicles - 1)
    local_source = (local_target + local_shift) % vesicles
    local_onehot = onehot(local_source, vesicles)
    local_terms = gather_pair_terms(
        jnp.ones((vesicles, 1), jnp.int32),
        local_target,
        local_source,
        near_flat,
        rows_per_vesicle,
        near_flat,
        rows_per_vesicle,
    )
    remote_terms = gather_pair_terms(
        live,
        jnp.asarray(pair_tile.astype(np.int32)),
        sources,
        incoming,
        tile,
        near_flat,
        rows_per_vesicle,
    )
    near_total = jnp.einsum(
        "pv,kpx->vkx", local_onehot, local_terms, precision=HIGHEST
    ) + jnp.einsum("pv,kpx->vkx", source_onehot, remote_terms, precision=HIGHEST)

    near_weighted = near_total.reshape(vesicles * 3, near_points) * jnp.asarray(
        near_quadrature.astype(np.float32)
    )
    gradient = gradient + lax.dot_general(
        near_weighted, near, contract_points, precision=HIGHEST
    ).reshape(cotangent.shape)

    coupling = jnp.asarray(far_coupling(REGIONS, vesicles * devices).astype(np.float32))
    far_field = lax.dot_general(coupling, far_total, contract_rows, precision=HIGHEST)
    far_terms = jnp.dot(member, far_field, precision=HIGHEST).reshape(vesicles, 3, FAR)
    return gradient + jnp.pad(far_terms, ((0, 0), (0, 0), (0, coef_count - FAR)))


def solution(mesh):
    in_specs = (
        P("dev", None, None),
        P("dev", None, None),
        P("dev"),
        P("dev"),
        P("dev"),
        P("dev", None, None),
        P("dev", None, None),
        P("dev", None),
    )
    out_specs = P("dev", None, None)
    return jax.shard_map(
        on_device, mesh=mesh, in_specs=in_specs, out_specs=out_specs, check_vma=False
    )
```

```python
import functools
import math

import jax
import jax.numpy as jnp
import numpy as np
from jax import lax
from jax.experimental import pallas as pl
from jax.experimental.pallas import tpu as pltpu
from jax.sharding import PartitionSpec as P

NLAT = 24
NEAR_LAT = 8
REGIONS = 64
FAR = 8


HIGHEST = lax.Precision.HIGHEST


def harmonic_tables(grid_lat, degree_count):
    longitudes = 2 * grid_lat
    full_longitudes = 2 * degree_count
    colatitude = (np.arange(grid_lat, dtype=np.float64) + 0.5) * (math.pi / grid_lat)
    cosine = np.cos(colatitude)
    values = [np.ones_like(cosine), cosine]
    for degree in range(2, degree_count):
        values.append(((2 * degree - 1) * cosine * values[-1] - (degree - 1) * values[-2]) / degree)
    degrees = np.arange(degree_count, dtype=np.float64)
    legendre = np.stack(values[:degree_count], axis=1) * np.sqrt((2.0 * degrees + 1.0) / 2.0)
    azimuth = np.arange(longitudes, dtype=np.float64) * (2.0 * math.pi / longitudes)
    halfway = degree_count // 2
    mode_index = np.arange(degree_count, dtype=np.float64)
    frequency = np.where(mode_index < halfway, mode_index, mode_index - halfway + 1.0)
    phases = azimuth[:, None] * frequency[None, :]
    fourier = np.where(mode_index[None, :] < halfway, np.cos(phases), np.sin(phases))
    fourier = fourier * np.where(
        mode_index[None, :] == 0, math.sqrt(1.0 / full_longitudes), math.sqrt(2.0 / full_longitudes)
    )
    synthesis = np.einsum("jl,km->lmjk", legendre, fourier).reshape(
        degree_count * degree_count, grid_lat * longitudes
    )
    quadrature = np.repeat(np.sin(colatitude) * (math.pi / grid_lat), longitudes)
    degree_scale = np.repeat(1.0 / (2.0 * degrees + 1.0), degree_count)
    return (synthesis, quadrature, degree_scale)


def far_coupling(regions, vesicle_total):
    position = np.arange(regions, dtype=np.float64)
    return 1.0 / ((1.0 + np.abs(position[:, None] - position[None, :])) * math.sqrt(vesicle_total))


GROUP = 8

def gather_pair_kernel(t_stride, s_stride, live_ref, tidx_ref, sidx_ref, *refs):
    t_ref, s_ref, o_ref, order_ref, tile_ref, cot_ref = refs
    pairs = live_ref.shape[0]
    scale = 1.0 / math.sqrt(t_ref.shape[1])
    o_ref[...] = jnp.zeros(o_ref.shape, o_ref.dtype)
    cot_ref[...] = jnp.zeros(cot_ref.shape, cot_ref.dtype)

    def pack(p, count):
        order_ref[count] = p
        return count + live_ref[p]

    count = lax.fori_loop(0, pairs, pack, 0, unroll=8)
    for j in range(GROUP):
        order_ref[count + j] = order_ref[0]

    def group_body(g, carry):
        picked = [order_ref[g * GROUP + j] for j in range(GROUP)]
        for j in range(GROUP):
            t_row = (picked[j] if tidx_ref is None else tidx_ref[picked[j]]) * t_stride
            s_row = sidx_ref[picked[j]] * s_stride
            for c in range(3):
                tile_ref[c, pl.ds(j, 1), :] = t_ref[pl.ds(t_row + c, 1), :]
                cot_ref[j, pl.ds(c, 1), :] = t_ref[pl.ds(t_row + 3 + c, 1), :]
                tile_ref[3 + c, pl.ds(j, 1), :] = s_ref[pl.ds(s_row + c, 1), :]
        t_cols = [tile_ref[c].T for c in range(3)]
        s_rows = [tile_ref[3 + c] for c in range(3)]
        for p in range(GROUP):
            distance = None
            for c in range(3):
                apart = t_cols[c][:, p : p + 1] - s_rows[c][p : p + 1, :]
                distance = apart * apart if distance is None else distance + apart * apart
            kernel_block = 1.0 / (1.0 + distance)
            terms = jnp.dot(
                cot_ref[p], kernel_block, precision=HIGHEST, preferred_element_type=jnp.float32
            )
            for c in range(3):
                o_ref[c, pl.ds(picked[p], 1), :] = terms[c : c + 1, :] * scale
        return carry

    lax.fori_loop(0, (count + GROUP - 1) // GROUP, group_body, 0)


def gather_pair_terms(live, target_index, source_index, target_rows, t_stride, source_rows, s_stride):
    pairs = live.shape[0]
    points = target_rows.shape[1]
    vmem = pl.BlockSpec(memory_space=pltpu.VMEM)
    smem = pl.BlockSpec(memory_space=pltpu.SMEM)
    kernel = functools.partial(gather_pair_kernel, t_stride, s_stride)
    if target_index is None:
        indices = (live, source_index)
        body = lambda live_ref, sidx_ref, *refs: kernel(live_ref, None, sidx_ref, *refs)
    else:
        indices = (live, target_index, source_index)
        body = kernel
    return pl.pallas_call(
        body,
        in_specs=[smem] * len(indices) + [vmem, vmem],
        out_specs=vmem,
        out_shape=jax.ShapeDtypeStruct((3, pairs, points), jnp.float32),
        scratch_shapes=[
            pltpu.SMEM((pairs + GROUP,), jnp.int32),
            pltpu.VMEM((6, GROUP, points), jnp.float32),
            pltpu.VMEM((GROUP, 8, points), jnp.float32),
        ],
        name="gather_pair_terms",
    )(*indices, target_rows, source_rows)


def onehot(index, count):
    return (index[:, None] == jnp.arange(count, dtype=jnp.int32)[None, :]).astype(jnp.float32)


def on_device(
    cotangent, surface, region_id, local_target, local_shift, near_target, near_source, near_count
):
    vesicles = cotangent.shape[0]
    coef_count = cotangent.shape[2]
    devices = lax.axis_size("dev")
    slot_count = near_target.shape[2]
    pair_slots = devices * slot_count

    synthesis, quadrature, degree_scale = harmonic_tables(NLAT, NLAT)
    near_synthesis, near_quadrature, unused_scale = harmonic_tables(NEAR_LAT, NLAT)
    points = synthesis.shape[1]
    near_points = near_synthesis.shape[1]
    full = jnp.asarray(synthesis.astype(np.float32))
    near = jnp.asarray(near_synthesis.astype(np.float32))
    contract_rows = (((0,), (0,)), ((), ()))
    cot_flat = cotangent.reshape(vesicles * 3, coef_count)
    surface_flat = surface.reshape(vesicles * 3, coef_count)

    picks_low = np.eye(coef_count, FAR, dtype=np.float32)
    near_and_low = jnp.asarray(np.concatenate([near_synthesis.astype(np.float32), picks_low], 1))
    cot_near_low = jnp.dot(cot_flat, near_and_low, precision=HIGHEST)
    near_cot = cot_near_low[:, :near_points].reshape(vesicles, 3, near_points)
    moments = cot_near_low[:, near_points:].reshape(vesicles, 3 * FAR)
    near_shape = jnp.dot(surface_flat, near, precision=HIGHEST).reshape(vesicles, 3, near_points)
    cot_points = jnp.dot(cot_flat, full, precision=HIGHEST).reshape(vesicles, 3, points)
    shape_points = jnp.dot(surface_flat, full, precision=HIGHEST).reshape(vesicles, 3, points)
    stretch = 1.0 / (1.0 + jnp.sum(shape_points * shape_points, axis=1))
    point_total = stretch[:, None, :] * cot_points * jnp.asarray(quadrature.astype(np.float32))
    contract_points = (((1,), (1,)), ((), ()))
    point_coefs = lax.dot_general(
        point_total.reshape(vesicles * 3, points), full, contract_points, precision=HIGHEST
    )
    gradient = lax.optimization_barrier(
        jnp.asarray(degree_scale.astype(np.float32)) * cotangent
        + point_coefs.reshape(cotangent.shape)
    )

    near_vkx = jnp.concatenate([near_shape, near_cot], axis=1)
    rows_per_vesicle = near_vkx.shape[1]
    near_flat = near_vkx.reshape(vesicles * rows_per_vesicle, near_points)

    targets = near_target[0].reshape(pair_slots)
    alive = (
        jnp.arange(slot_count, dtype=jnp.int32)[None, :] < near_count[0][:, None]
    ).reshape(pair_slots)
    picked = jnp.einsum("pv,vkx->pkx", onehot(targets, vesicles), near_vkx, precision=HIGHEST)
    kind = jnp.arange(rows_per_vesicle, dtype=jnp.int32)[None, :, None]
    picked = jnp.where((kind < 3) | alive[:, None, None], picked, 0.0)
    member = onehot(region_id, REGIONS)
    partial_far = lax.dot_general(member, moments, contract_rows, precision=HIGHEST)
    far_rows = REGIONS * 3 * FAR // (slot_count * near_points)
    far_block = partial_far.reshape(1, slot_count, far_rows, near_points)
    far_block = jnp.broadcast_to(far_block, (devices, slot_count, far_rows, near_points))
    pair_rows = rows_per_vesicle + far_rows
    outgoing = jnp.concatenate(
        [picked, far_block.reshape(pair_slots, far_rows, near_points)], axis=1
    ).reshape(pair_slots * pair_rows, near_points)
    incoming = lax.all_to_all(outgoing, "dev", split_axis=0, concat_axis=0, tiled=True)
    peer_rows = jnp.sum(incoming.reshape(devices, slot_count * pair_rows, near_points), axis=0)
    far_total = peer_rows.reshape(slot_count, pair_rows, near_points)[:, rows_per_vesicle:, :]
    far_total = far_total.reshape(REGIONS, 3 * FAR)
    sources = jnp.clip(near_source[0].reshape(pair_slots), 0, vesicles - 1)
    source_onehot = onehot(sources, vesicles)

    local_target = jnp.clip(local_target, 0, vesicles - 1)
    local_source = (local_target + local_shift) % vesicles
    local_onehot = onehot(local_source, vesicles)
    local_terms = gather_pair_terms(
        jnp.ones((vesicles,), jnp.int32),
        local_target,
        local_source,
        near_flat,
        rows_per_vesicle,
        near_flat,
        rows_per_vesicle,
    )
    row_size = jnp.max(jnp.abs(incoming), axis=1).reshape(pair_slots, pair_rows)
    live = (jnp.max(row_size[:, 3:rows_per_vesicle], axis=1) > 0.0).astype(jnp.int32)
    remote_terms = gather_pair_terms(
        live,
        None,
        sources,
        incoming,
        pair_rows,
        near_flat,
        rows_per_vesicle,
    )
    near_total = jnp.einsum(
        "pv,kpx->vkx", local_onehot, local_terms, precision=HIGHEST
    ) + jnp.einsum("pv,kpx->vkx", source_onehot, remote_terms, precision=HIGHEST)

    near_weighted = near_total.reshape(vesicles * 3, near_points) * jnp.asarray(
        near_quadrature.astype(np.float32)
    )
    gradient = gradient + lax.dot_general(
        near_weighted, near, contract_points, precision=HIGHEST
    ).reshape(cotangent.shape)

    coupling = jnp.asarray(far_coupling(REGIONS, vesicles * devices).astype(np.float32))
    far_field = lax.dot_general(coupling, far_total, contract_rows, precision=HIGHEST)
    far_terms = jnp.dot(member, far_field, precision=HIGHEST).reshape(vesicles, 3, FAR)
    return gradient + jnp.pad(far_terms, ((0, 0), (0, 0), (0, coef_count - FAR)))


def solution(mesh):
    in_specs = (
        P("dev", None, None),
        P("dev", None, None),
        P("dev"),
        P("dev"),
        P("dev"),
        P("dev", None, None),
        P("dev", None, None),
        P("dev", None),
    )
    out_specs = P("dev", None, None)
    return jax.shard_map(
        on_device, mesh=mesh, in_specs=in_specs, out_specs=out_specs, check_vma=False
    )
```

```python
import functools
import math

import jax
import jax.numpy as jnp
import numpy as np
from jax import lax
from jax.experimental import pallas as pl
from jax.experimental.pallas import tpu as pltpu
from jax.sharding import PartitionSpec as P

NLAT = 24
NEAR_LAT = 8
REGIONS = 64
FAR = 8


HIGHEST = lax.Precision.HIGHEST


def harmonic_tables(grid_lat, degree_count):
    longitudes = 2 * grid_lat
    full_longitudes = 2 * degree_count
    colatitude = (np.arange(grid_lat, dtype=np.float64) + 0.5) * (math.pi / grid_lat)
    cosine = np.cos(colatitude)
    values = [np.ones_like(cosine), cosine]
    for degree in range(2, degree_count):
        values.append(((2 * degree - 1) * cosine * values[-1] - (degree - 1) * values[-2]) / degree)
    degrees = np.arange(degree_count, dtype=np.float64)
    legendre = np.stack(values[:degree_count], axis=1) * np.sqrt((2.0 * degrees + 1.0) / 2.0)
    azimuth = np.arange(longitudes, dtype=np.float64) * (2.0 * math.pi / longitudes)
    halfway = degree_count // 2
    mode_index = np.arange(degree_count, dtype=np.float64)
    frequency = np.where(mode_index < halfway, mode_index, mode_index - halfway + 1.0)
    phases = azimuth[:, None] * frequency[None, :]
    fourier = np.where(mode_index[None, :] < halfway, np.cos(phases), np.sin(phases))
    fourier = fourier * np.where(
        mode_index[None, :] == 0, math.sqrt(1.0 / full_longitudes), math.sqrt(2.0 / full_longitudes)
    )
    synthesis = np.einsum("jl,km->lmjk", legendre, fourier).reshape(
        degree_count * degree_count, grid_lat * longitudes
    )
    quadrature = np.repeat(np.sin(colatitude) * (math.pi / grid_lat), longitudes)
    degree_scale = np.repeat(1.0 / (2.0 * degrees + 1.0), degree_count)
    return (synthesis, quadrature, degree_scale)


def far_coupling(regions, vesicle_total):
    position = np.arange(regions, dtype=np.float64)
    return 1.0 / ((1.0 + np.abs(position[:, None] - position[None, :])) * math.sqrt(vesicle_total))


GROUP = 8

def gather_pair_kernel(t_stride, s_stride, live_ref, tidx_ref, sidx_ref, *refs):
    t_ref, s_ref, o_ref, order_ref, tile_ref, cot_ref = refs
    pairs = live_ref.shape[0]
    scale = 1.0 / math.sqrt(t_ref.shape[1])
    o_ref[...] = jnp.zeros(o_ref.shape, o_ref.dtype)
    cot_ref[...] = jnp.zeros(cot_ref.shape, cot_ref.dtype)

    def pack(p, count):
        order_ref[count] = p
        return count + live_ref[p]

    count = lax.fori_loop(0, pairs, pack, 0, unroll=8)
    for j in range(GROUP):
        order_ref[count + j] = order_ref[0]

    def group_body(g, carry):
        picked = [order_ref[g * GROUP + j] for j in range(GROUP)]
        for j in range(GROUP):
            t_row = (picked[j] if tidx_ref is None else tidx_ref[picked[j]]) * t_stride
            s_row = sidx_ref[picked[j]] * s_stride
            for c in range(3):
                tile_ref[c, pl.ds(j, 1), :] = t_ref[pl.ds(t_row + c, 1), :]
                cot_ref[j, pl.ds(c, 1), :] = t_ref[pl.ds(t_row + 3 + c, 1), :]
                tile_ref[3 + c, pl.ds(j, 1), :] = s_ref[pl.ds(s_row + c, 1), :]
        t_cols = [tile_ref[c].T for c in range(3)]
        s_rows = [tile_ref[3 + c] for c in range(3)]
        for p in range(GROUP):
            distance = None
            for c in range(3):
                apart = t_cols[c][:, p : p + 1] - s_rows[c][p : p + 1, :]
                distance = apart * apart if distance is None else distance + apart * apart
            kernel_block = 1.0 / (1.0 + distance)
            terms = jnp.dot(
                cot_ref[p], kernel_block, precision=HIGHEST, preferred_element_type=jnp.float32
            )
            for c in range(3):
                o_ref[c, pl.ds(picked[p], 1), :] = terms[c : c + 1, :] * scale
        return carry

    lax.fori_loop(0, (count + GROUP - 1) // GROUP, group_body, 0)


def gather_pair_terms(live, target_index, source_index, target_rows, t_stride, source_rows, s_stride):
    pairs = live.shape[0]
    points = target_rows.shape[1]
    vmem = pl.BlockSpec(memory_space=pltpu.VMEM)
    smem = pl.BlockSpec(memory_space=pltpu.SMEM)
    kernel = functools.partial(gather_pair_kernel, t_stride, s_stride)
    if target_index is None:
        indices = (live, source_index)
        body = lambda live_ref, sidx_ref, *refs: kernel(live_ref, None, sidx_ref, *refs)
    else:
        indices = (live, target_index, source_index)
        body = kernel
    return pl.pallas_call(
        body,
        in_specs=[smem] * len(indices) + [vmem, vmem],
        out_specs=vmem,
        out_shape=jax.ShapeDtypeStruct((3, pairs, points), jnp.float32),
        scratch_shapes=[
            pltpu.SMEM((pairs + GROUP,), jnp.int32),
            pltpu.VMEM((6, GROUP, points), jnp.float32),
            pltpu.VMEM((GROUP, 8, points), jnp.float32),
        ],
        name="gather_pair_terms",
    )(*indices, target_rows, source_rows)


def onehot(index, count):
    return (index[:, None] == jnp.arange(count, dtype=jnp.int32)[None, :]).astype(jnp.float32)


def separable_table(grid_lat, degree_count):
    longitudes = 2 * grid_lat
    full_longitudes = 2 * degree_count
    colatitude = (np.arange(grid_lat, dtype=np.float64) + 0.5) * (math.pi / grid_lat)
    cosine = np.cos(colatitude)
    values = [np.ones_like(cosine), cosine]
    for degree in range(2, degree_count):
        values.append(((2 * degree - 1) * cosine * values[-1] - (degree - 1) * values[-2]) / degree)
    degrees = np.arange(degree_count, dtype=np.float64)
    legendre = np.stack(values[:degree_count], axis=1) * np.sqrt((2.0 * degrees + 1.0) / 2.0)
    azimuth = np.arange(longitudes, dtype=np.float64) * (2.0 * math.pi / longitudes)
    halfway = degree_count // 2
    mode_index = np.arange(degree_count, dtype=np.float64)
    frequency = np.where(mode_index < halfway, mode_index, mode_index - halfway + 1.0)
    phases = azimuth[:, None] * frequency[None, :]
    fourier = np.where(mode_index[None, :] < halfway, np.cos(phases), np.sin(phases))
    fourier = fourier * np.where(
        mode_index[None, :] == 0, math.sqrt(1.0 / full_longitudes), math.sqrt(2.0 / full_longitudes)
    )
    leg_t, four_t = lax.optimization_barrier(
        (jnp.asarray(legendre.T.astype(np.float32)), jnp.asarray(fourier.T.astype(np.float32)))
    )
    rows = jnp.arange(degree_count * degree_count, dtype=jnp.int32)
    cols = jnp.arange(grid_lat * longitudes, dtype=jnp.int32)
    row_l = onehot(rows // degree_count, degree_count)
    row_m = onehot(rows % degree_count, degree_count)
    col_j = onehot(cols // longitudes, grid_lat).T
    col_k = onehot(cols % longitudes, longitudes).T
    spread_l = jnp.dot(jnp.dot(row_l, leg_t, precision=HIGHEST), col_j, precision=HIGHEST)
    spread_m = jnp.dot(jnp.dot(row_m, four_t, precision=HIGHEST), col_k, precision=HIGHEST)
    return spread_l * spread_m


def on_device(
    cotangent, surface, region_id, local_target, local_shift, near_target, near_source, near_count
):
    vesicles = cotangent.shape[0]
    coef_count = cotangent.shape[2]
    devices = lax.axis_size("dev")
    slot_count = near_target.shape[2]
    pair_slots = devices * slot_count

    synthesis, quadrature, degree_scale = harmonic_tables(NLAT, NLAT)
    near_synthesis, near_quadrature, unused_scale = harmonic_tables(NEAR_LAT, NLAT)
    points = synthesis.shape[1]
    near_points = near_synthesis.shape[1]
    full = separable_table(NLAT, NLAT)
    near = jnp.asarray(near_synthesis.astype(np.float32))
    contract_rows = (((0,), (0,)), ((), ()))
    cot_flat = cotangent.reshape(vesicles * 3, coef_count)
    surface_flat = surface.reshape(vesicles * 3, coef_count)

    near_cot = jnp.dot(cot_flat, near, precision=HIGHEST).reshape(vesicles, 3, near_points)
    near_shape = jnp.dot(surface_flat, near, precision=HIGHEST).reshape(vesicles, 3, near_points)
    cot_points = jnp.dot(cot_flat, full, precision=HIGHEST).reshape(vesicles, 3, points)
    shape_points = jnp.dot(surface_flat, full, precision=HIGHEST).reshape(vesicles, 3, points)
    stretch = 1.0 / (1.0 + jnp.sum(shape_points * shape_points, axis=1))
    point_total = stretch[:, None, :] * cot_points * jnp.asarray(quadrature.astype(np.float32))
    contract_points = (((1,), (1,)), ((), ()))
    point_coefs = lax.dot_general(
        point_total.reshape(vesicles * 3, points), full, contract_points, precision=HIGHEST
    )
    gradient = lax.optimization_barrier(
        jnp.asarray(degree_scale.astype(np.float32)) * cotangent
        + point_coefs.reshape(cotangent.shape)
    )

    near_vkx = jnp.concatenate([near_shape, near_cot], axis=1)
    rows_per_vesicle = near_vkx.shape[1]
    near_flat = near_vkx.reshape(vesicles * rows_per_vesicle, near_points)

    targets = near_target[0].reshape(pair_slots)
    alive = (
        jnp.arange(slot_count, dtype=jnp.int32)[None, :] < near_count[0][:, None]
    ).reshape(pair_slots)
    picked = jnp.einsum("pv,vkx->pkx", onehot(targets, vesicles), near_vkx, precision=HIGHEST)
    kind = jnp.arange(rows_per_vesicle, dtype=jnp.int32)[None, :, None]
    picked = jnp.where((kind < 3) | alive[:, None, None], picked, 0.0)
    member = onehot(region_id, REGIONS)
    partial_far = lax.dot_general(
        member, cot_flat.reshape(vesicles, 3 * coef_count), contract_rows, precision=HIGHEST
    ).reshape(REGIONS, 3, coef_count)[:, :, :FAR].reshape(REGIONS, 3 * FAR)
    far_rows = REGIONS * 3 * FAR // (slot_count * near_points)
    far_block = partial_far.reshape(1, slot_count, far_rows, near_points)
    far_block = jnp.broadcast_to(far_block, (devices, slot_count, far_rows, near_points))
    pair_rows = rows_per_vesicle + far_rows
    outgoing = jnp.concatenate(
        [picked, far_block.reshape(pair_slots, far_rows, near_points)], axis=1
    ).reshape(pair_slots * pair_rows, near_points)
    incoming = lax.all_to_all(outgoing, "dev", split_axis=0, concat_axis=0, tiled=True)
    peer_rows = jnp.sum(incoming.reshape(devices, slot_count * pair_rows, near_points), axis=0)
    far_total = peer_rows.reshape(slot_count, pair_rows, near_points)[:, rows_per_vesicle:, :]
    far_total = far_total.reshape(REGIONS, 3 * FAR)
    sources = jnp.clip(near_source[0].reshape(pair_slots), 0, vesicles - 1)
    source_onehot = onehot(sources, vesicles)

    local_target = jnp.clip(local_target, 0, vesicles - 1)
    local_source = (local_target + local_shift) % vesicles
    local_onehot = onehot(local_source, vesicles)
    local_terms = gather_pair_terms(
        jnp.ones((vesicles,), jnp.int32),
        local_target,
        local_source,
        near_flat,
        rows_per_vesicle,
        near_flat,
        rows_per_vesicle,
    )
    row_size = jnp.max(jnp.abs(incoming), axis=1).reshape(pair_slots, pair_rows)
    live = (jnp.max(row_size[:, 3:rows_per_vesicle], axis=1) > 0.0).astype(jnp.int32)
    remote_terms = gather_pair_terms(
        live,
        None,
        sources,
        incoming,
        pair_rows,
        near_flat,
        rows_per_vesicle,
    )
    near_total = jnp.einsum(
        "pv,kpx->vkx", local_onehot, local_terms, precision=HIGHEST
    ) + jnp.einsum("pv,kpx->vkx", source_onehot, remote_terms, precision=HIGHEST)

    near_weighted = near_total.reshape(vesicles * 3, near_points) * jnp.asarray(
        near_quadrature.astype(np.float32)
    )
    gradient = gradient + lax.dot_general(
        near_weighted, near, contract_points, precision=HIGHEST
    ).reshape(cotangent.shape)

    coupling = jnp.asarray(far_coupling(REGIONS, vesicles * devices).astype(np.float32))
    far_field = lax.dot_general(coupling, far_total, contract_rows, precision=HIGHEST)
    far_terms = jnp.dot(member, far_field, precision=HIGHEST).reshape(vesicles, 3, FAR)
    return gradient + jnp.pad(far_terms, ((0, 0), (0, 0), (0, coef_count - FAR)))


def solution(mesh):
    in_specs = (
        P("dev", None, None),
        P("dev", None, None),
        P("dev"),
        P("dev"),
        P("dev"),
        P("dev", None, None),
        P("dev", None, None),
        P("dev", None),
    )
    out_specs = P("dev", None, None)
    return jax.shard_map(
        on_device, mesh=mesh, in_specs=in_specs, out_specs=out_specs, check_vma=False
    )
```
